32 devices in a mesh: groups: 2 (over y), seq: 4 (over z), head: 4 (over x, core).
Axes of the slice: x: 2, y: 2, z: 4, core: 2. Of those that a mesh axis runs over, the one named last changes fastest.
Arguments:
- queries: bfloat16 [1024, 16, 128], P(('groups', 'seq'), 'head'), parts along dimension 0, may hold values from -1.25 to 1.25
- reflect_keys: bfloat16 [1024, 2, 16, 128], P(('groups', 'seq'), None, 'head'), parts along dimension 0, may hold values from -1.25 to 1.25
- write_values: bfloat16 [1024, 2, 16, 128], P(('groups', 'seq'), None, 'head'), parts along dimension 0, may hold values from -2.5 to 2.5
- out_cotangent: bfloat16 [1024, 16, 128], P(('groups', 'seq'), 'head'), parts along dimension 0, may hold values from -4 to 4
Outputs:
- outputs: bfloat16 [1024, 16, 128], P(('groups', 'seq'), 'head'), parts along dimension 0
- grad_queries: bfloat16 [1024, 16, 128], P(('groups', 'seq'), 'head'), parts along dimension 0
- grad_keys: bfloat16 [1024, 2, 16, 128], P(('groups', 'seq'), None, 'head'), parts along dimension 0
- grad_values: bfloat16 [1024, 2, 16, 128], P(('groups', 'seq'), None, 'head'), parts along dimension 0
The draws below stay inside these ranges and needn't reach their ends.
There are 2 independent parts, one for each index of `groups`. The reference program is written for one: setup_inputs(seed, part) draws one part's arguments, and reference() takes and returns one part's arrays. A program takes and returns all parts, laid end to end along the dimension named above; each array names one. Nothing has to cross between parts.
All inputs are finite; a program needn't handle non-finite values.
Results may differ from the reference program's by a relative error of at most 0.0012.
Values sent between devices are 32-bit elements; how exact they have to be, the bound alone decides.
No kernel may reach another device: no remote copies, remote signals or barrier semaphores. Data moves between devices by JAX's collectives and lax.ppermute only.
A program may use at most 128 MiB of HBM per device.

```python
import jax
import jax.numpy as jnp
from jax import lax

HEADS = 16
DK = 128
BLK = 128
TOK_DEV = 128
TOKENS = 512
N_SEQ = 4


def block_scale(key, shape, cuts, low, largest):
    loudness = 1.0
    for position, shards_of in cuts:
        steps = jax.random.uniform(jax.random.fold_in(jax.random.fold_in(key, 6), position), (shards_of,), jnp.float32, low / len(cuts), largest / len(cuts))
        loudness = loudness * jnp.repeat(jnp.exp(steps), shape[position] // shards_of).reshape((-1,) + (1,) * (len(shape) - 1 - position))
    return loudness


def centred(stream_key, extent, width, most, cuts=(), held_as=jnp.bfloat16):
    entries = jax.random.normal(stream_key, extent, jnp.float32) * width
    if len(cuts) > 0:
        entries = block_scale(stream_key, extent, cuts, -0.22, 0.18) * entries
    return jnp.clip(entries, min=-most, max=most).astype(held_as)


def setup_inputs(seed: int = 0, part: int = 0) -> dict:
    seeds = jax.random.split(jax.random.key(seed), 5)
    part_splits = jax.random.split(jax.random.fold_in(seeds[4], part), 5)
    return {
        "queries": centred(part_splits[0], (TOKENS, HEADS, DK), (DK ** -0.5), 1.25, ((0, 4), (1, 4))),
        "reflect_keys": centred(part_splits[1], (TOKENS, 2, HEADS, DK), (DK ** -0.5), 1.25, ((0, 4), (2, 4))),
        "write_values": centred(part_splits[2], (TOKENS, 2, HEADS, DK), (4 * TOKENS ** -0.5), 2.5, ((0, 4), (2, 4))),
        "out_cotangent": centred(part_splits[3], (TOKENS, HEADS, DK), (6 * TOKENS ** -0.5), 4.0, ((0, 4), (1, 4))),
    }


highest = lax.Precision.HIGHEST

def unit_rows(tensor):
    return tensor * lax.rsqrt(lax.optimization_barrier(jnp.sum(tensor * tensor, axis=-1, keepdims=True)) + 1e-06)

def batch_product(left, right):
    return jnp.einsum('hij,hjk->hik', left, right, precision=highest)

def lower_inverse(system):
    row_count = system.shape[1]
    if row_count <= 16:
        eye_part = jnp.eye(row_count, dtype=jnp.float32)
        power = eye_part - system
        inverse = eye_part + power
        reach = 2
        while reach < row_count:
            power = batch_product(power, power)
            inverse = inverse + batch_product(inverse, power)
            reach = reach * 2
        return inverse
    half = row_count // 2
    upper_inv = lower_inverse(system[:, :half, :half])
    lower_inv = lower_inverse(system[:, half:, half:])
    corner = -batch_product(lower_inv, batch_product(system[:, half:, :half], upper_inv))
    top = jnp.concatenate([upper_inv, jnp.zeros_like(upper_inv)], axis=2)
    bottom = jnp.concatenate([corner, lower_inv], axis=2)
    return jnp.concatenate([top, bottom], axis=1)

def block_step(carried, pieces):
    query_blk, key_blk, value_blk = pieces
    row_count = key_blk.shape[0]
    tok_count = query_blk.shape[0]
    key_gram = jnp.einsum('ihd,jhd->hij', key_blk, key_blk, precision=highest)
    row_ids = lax.broadcasted_iota(jnp.int32, (row_count, row_count), 0)
    col_ids = lax.broadcasted_iota(jnp.int32, (row_count, row_count), 1)
    system = jnp.eye(row_count, dtype=jnp.float32) + jnp.where(row_ids > col_ids, 2.0 * key_gram, jnp.float32(0.0))
    target = value_blk - jnp.einsum('ihd,hdw->ihw', key_blk, carried, precision=highest)
    updates = jnp.einsum('hij,jhw->ihw', lower_inverse(system), target, precision=highest)
    scores = 2.0 * jnp.einsum('ihd,jhd->hij', query_blk, key_blk, precision=highest)
    tok_ids = lax.broadcasted_iota(jnp.int32, (tok_count, row_count), 0)
    sub_ids = lax.broadcasted_iota(jnp.int32, (tok_count, row_count), 1)
    visible = sub_ids <= 2 * tok_ids + 1
    result = jnp.einsum('ihd,hdw->ihw', query_blk, carried, precision=highest)
    result = result + jnp.einsum('hij,jhw->ihw', jnp.where(visible, scores, jnp.float32(0.0)), updates, precision=highest)
    carried = carried + 2.0 * jnp.einsum('ihd,ihw->hdw', key_blk, updates, precision=highest)
    return (carried, result)

def stretch_run(initial, query_rows, key_rows, value_rows):
    tok_count, heads_here, head_size = query_rows.shape
    blocks = tok_count // BLK

    def split_blocks(tensor, row_span):
        return tensor.reshape(blocks, row_span, tensor.shape[1], tensor.shape[2])
    last_state, pieces = lax.scan(block_step, initial, (split_blocks(query_rows, BLK), split_blocks(key_rows, 2 * BLK), split_blocks(value_rows, 2 * BLK)))
    merged = pieces.reshape(tok_count, heads_here, pieces.shape[3])
    return (merged, last_state)

def local_layer(initial, query_in, key_in, value_in):
    return stretch_run(initial, unit_rows(query_in), unit_rows(key_in), value_in)

def reference(queries, reflect_keys, write_values, out_cotangent):
    stretches = N_SEQ
    query_c = queries.astype(jnp.float32).reshape(stretches, TOK_DEV, HEADS, DK)
    cot_c = out_cotangent.astype(jnp.float32).reshape(stretches, TOK_DEV, HEADS, DK)
    key_c = reflect_keys.astype(jnp.float32).reshape(stretches, 2 * TOK_DEV, HEADS, DK)
    value_c = write_values.astype(jnp.float32).reshape(stretches, 2 * TOK_DEV, HEADS, DK)
    zero_state = jnp.zeros((HEADS, DK, DK), jnp.float32)

    def advance(carried, inputs):
        query_in, key_in, value_in = inputs
        produced, last_state = local_layer(carried, query_in, key_in, value_in)
        return (last_state, (produced, carried))
    unused, (produced_all, starts) = lax.scan(advance, zero_state, (query_c, key_c, value_c))

    def retreat(cot_state, inputs):
        query_in, key_in, value_in, cot_in, state_in = inputs
        unused_out, pull_back = jax.vjp(local_layer, state_in, query_in, key_in, value_in)
        d_state, d_query, d_key, d_value = pull_back((cot_in, cot_state))
        return (d_state, (d_query, d_key, d_value))
    unused_cot, (grads_q, grads_k, grads_v) = lax.scan(retreat, zero_state, (query_c, key_c, value_c, cot_c, starts), reverse=True)

    def token_major(tensor):
        return tensor.reshape(TOKENS, HEADS, DK).astype(jnp.bfloat16)

    def pair_major(tensor):
        return tensor.reshape(TOKENS, 2, HEADS, DK).astype(jnp.bfloat16)
    return (token_major(produced_all), token_major(grads_q), pair_major(grads_k), pair_major(grads_v))
```

```python
import jax
import jax.numpy as jnp
from jax import lax
from jax.sharding import PartitionSpec as P

highest = lax.Precision.HIGHEST
LEAF = 16


def mm(spec, *operands):
    return jnp.einsum(spec, *operands, precision=highest)


def unit_rows(tensor):
    scale = lax.rsqrt(jnp.sum(tensor * tensor, axis=-1, keepdims=True) + 1e-06)
    return tensor * scale, scale


def strict_lower(rows, cols):
    return lax.broadcasted_iota(jnp.int32, (rows, cols), 0) > lax.broadcasted_iota(
        jnp.int32, (rows, cols), 1
    )


def tri_inverse(keys):
    heads, rows, size = keys.shape
    leaves = rows // LEAF
    leaf_keys = keys.reshape(heads, leaves, LEAF, size)
    gram = mm("hpid,hpjd->hpij", leaf_keys, leaf_keys)
    power = jnp.where(strict_lower(LEAF, LEAF), -2.0 * gram, 0.0)
    eye = jnp.eye(LEAF, dtype=jnp.float32)
    inverse = eye + power
    reach = 2
    while reach < LEAF:
        power = mm("hpij,hpjk->hpik", power, power)
        inverse = inverse + mm("hpij,hpjk->hpik", inverse, power)
        reach *= 2
    span = LEAF
    while span < rows:
        pairs = rows // (2 * span)
        blocks = inverse.reshape(heads, pairs, 2, span, span)
        upper_inv = blocks[:, :, 0]
        lower_inv = blocks[:, :, 1]
        halves = keys.reshape(heads, pairs, 2, span, size)
        link = 2.0 * mm("hpid,hpjd->hpij", halves[:, :, 1], halves[:, :, 0])
        corner = -mm("hpij,hpjk->hpik", lower_inv, mm("hpij,hpjk->hpik", link, upper_inv))
        top = jnp.concatenate([upper_inv, jnp.zeros_like(upper_inv)], axis=3)
        bottom = jnp.concatenate([corner, lower_inv], axis=3)
        inverse = jnp.concatenate([top, bottom], axis=2)
        span *= 2
    return inverse.reshape(heads, rows, rows)


def scan_seq(transition, offset, local_cot):
    count = lax.axis_size("seq")
    fwd_map, fwd_sum = transition, offset
    bwd_map, bwd_sum = transition, local_cot
    shift = 1
    while shift < count:
        right = [(i, i + shift) for i in range(count - shift)]
        left = [(i + shift, i) for i in range(count - shift)]
        last = 2 * shift >= count
        if last:
            got_sum = lax.ppermute(fwd_sum, "seq", right)
            got_cot = lax.ppermute(bwd_sum, "seq", left)
        else:
            got_map, got_sum = lax.ppermute((fwd_map, fwd_sum), "seq", right)
            got_bmap, got_cot = lax.ppermute((bwd_map, bwd_sum), "seq", left)
        fwd_sum = mm("hij,hjk->hik", fwd_map, got_sum) + fwd_sum
        bwd_sum = mm("hji,hjk->hik", bwd_map, got_cot) + bwd_sum
        if not last:
            fwd_map = mm("hij,hjk->hik", fwd_map, got_map)
            bwd_map = mm("hij,hjk->hik", got_bmap, bwd_map)
        shift *= 2
    state_in = lax.ppermute(fwd_sum, "seq", [(i, i + 1) for i in range(count - 1)])
    end_cot = lax.ppermute(bwd_sum, "seq", [(i + 1, i) for i in range(count - 1)])
    return state_in, end_cot


def local(queries, reflect_keys, write_values, out_cotangent):
    tok_count, heads_here, head_size = queries.shape
    rows = 2 * tok_count
    q_raw = queries.astype(jnp.float32).transpose(1, 0, 2)
    cot = out_cotangent.astype(jnp.float32).transpose(1, 0, 2)
    k_raw = reflect_keys.astype(jnp.float32).reshape(rows, heads_here, head_size).transpose(1, 0, 2)
    vals = write_values.astype(jnp.float32).reshape(rows, heads_here, head_size).transpose(1, 0, 2)
    qn, q_scale = unit_rows(q_raw)
    kn, k_scale = unit_rows(k_raw)

    inverse = tri_inverse(kn)
    proj = mm("hij,hjd->hid", inverse, kn)
    upd_v = mm("hij,hjd->hid", inverse, vals)
    tok_ids = lax.broadcasted_iota(jnp.int32, (tok_count, rows), 0)
    sub_ids = lax.broadcasted_iota(jnp.int32, (tok_count, rows), 1)
    visible = sub_ids <= 2 * tok_ids + 1
    scores = jnp.where(visible, 2.0 * mm("hid,hjd->hij", qn, kn), 0.0)
    read_map = qn - mm("hij,hjd->hid", scores, proj)
    own_out = mm("hij,hjd->hid", scores, upd_v)
    eye = jnp.eye(head_size, dtype=jnp.float32)
    transition = eye - 2.0 * mm("hjd,hjw->hdw", kn, proj)
    offset = 2.0 * mm("hjd,hjw->hdw", kn, upd_v)
    local_cot = mm("hld,hlw->hdw", read_map, cot)

    state_in, end_cot = scan_seq(transition, offset, local_cot)

    produced = mm("hld,hdw->hlw", read_map, state_in) + own_out
    updates = upd_v - mm("hjd,hdw->hjw", proj, state_in)
    d_upd = mm("hij,hiw->hjw", scores, cot) + 2.0 * mm("hjd,hdw->hjw", kn, end_cot)
    d_w = mm("hij,hiw->hjw", inverse, d_upd)
    touch = jnp.where(visible, mm("hiw,hjw->hij", cot, updates), 0.0)
    d_qn = mm("hiw,hdw->hid", cot, state_in) + 2.0 * mm("hij,hjd->hid", touch, kn)
    gram_cot = jnp.where(strict_lower(rows, rows), -2.0 * mm("hiw,hjw->hij", d_w, updates), 0.0)
    d_kn = (
        2.0 * mm("hij,hid->hjd", touch, qn)
        + 2.0 * mm("hjw,hdw->hjd", updates, end_cot)
        - mm("hjw,hdw->hjd", d_w, state_in)
        + mm("hij,hjd->hid", gram_cot, kn)
        + mm("hji,hjd->hid", gram_cot, kn)
    )
    d_q = q_scale * (d_qn - jnp.sum(qn * d_qn, axis=-1, keepdims=True) * qn)
    d_k = k_scale * (d_kn - jnp.sum(kn * d_kn, axis=-1, keepdims=True) * kn)

    def token_major(tensor):
        return tensor.transpose(1, 0, 2).astype(jnp.bfloat16)

    def pair_major(tensor):
        return (
            tensor.reshape(heads_here, tok_count, 2, head_size)
            .transpose(1, 2, 0, 3)
            .astype(jnp.bfloat16)
        )

    return (token_major(produced), token_major(d_q), pair_major(d_k), pair_major(d_w))


def solution(mesh):
    in_specs = (
        P(("groups", "seq"), "head", None),
        P(("groups", "seq"), None, "head", None),
        P(("groups", "seq"), None, "head", None),
        P(("groups", "seq"), "head", None),
    )
    out_specs = (
        P(("groups", "seq"), "head", None),
        P(("groups", "seq"), "head", None),
        P(("groups", "seq"), None, "head", None),
        P(("groups", "seq"), None, "head", None),
    )
    return jax.shard_map(local, mesh=mesh, in_specs=in_specs, out_specs=out_specs, check_vma=False)
```

```python
import jax
import jax.numpy as jnp
from jax import lax
from jax.sharding import PartitionSpec as P

highest = lax.Precision.HIGHEST
LEAF = 16


def mm(spec, *operands):
    return jnp.einsum(spec, *operands, precision=highest)


def unit_rows(tensor):
    scale = lax.rsqrt(jnp.sum(tensor * tensor, axis=-1, keepdims=True) + 1e-06)
    return tensor * scale, scale


def strict_lower(rows, cols):
    return lax.broadcasted_iota(jnp.int32, (rows, cols), 0) > lax.broadcasted_iota(
        jnp.int32, (rows, cols), 1
    )


def tri_inverse(keys):
    heads, rows, size = keys.shape
    leaves = rows // LEAF
    leaf_keys = keys.reshape(heads, leaves, LEAF, size)
    gram = mm("hpid,hpjd->hpij", leaf_keys, leaf_keys)
    power = jnp.where(strict_lower(LEAF, LEAF), -2.0 * gram, 0.0)
    eye = jnp.eye(LEAF, dtype=jnp.float32)
    inverse = eye + power
    reach = 2
    while reach < LEAF:
        power = mm("hpij,hpjk->hpik", power, power)
        inverse = inverse + mm("hpij,hpjk->hpik", inverse, power)
        reach *= 2
    span = LEAF
    while span < rows:
        pairs = rows // (2 * span)
        blocks = inverse.reshape(heads, pairs, 2, span, span)
        upper_inv = blocks[:, :, 0]
        lower_inv = blocks[:, :, 1]
        halves = keys.reshape(heads, pairs, 2, span, size)
        link = 2.0 * mm("hpid,hpjd->hpij", halves[:, :, 1], halves[:, :, 0])
        corner = -mm("hpij,hpjk->hpik", lower_inv, mm("hpij,hpjk->hpik", link, upper_inv))
        top = jnp.concatenate([upper_inv, jnp.zeros_like(upper_inv)], axis=3)
        bottom = jnp.concatenate([corner, lower_inv], axis=3)
        inverse = jnp.concatenate([top, bottom], axis=2)
        span *= 2
    return inverse.reshape(heads, rows, rows)


def chain_seq(transition, offset, local_cot):
    count = lax.axis_size("seq")
    right = [(i, i + 1) for i in range(count - 1)]
    left = [(i + 1, i) for i in range(count - 1)]
    fwd_sum, bwd_sum = offset, local_cot
    for hop in range(count - 1):
        got_sum = lax.ppermute(fwd_sum, "seq", right)
        got_cot = lax.ppermute(bwd_sum, "seq", left)
        if hop == count - 2:
            return got_sum, got_cot
        fwd_sum = mm("hij,hjk->hik", transition, got_sum) + offset
        bwd_sum = mm("hji,hjk->hik", transition, got_cot) + local_cot
    zero = jnp.zeros_like(offset)
    return zero, zero


def scan_seq(transition, offset, local_cot):
    count = lax.axis_size("seq")
    if count <= 4:
        return chain_seq(transition, offset, local_cot)
    fwd_map, fwd_sum = transition, offset
    bwd_map, bwd_sum = transition, local_cot
    shift = 1
    while shift < count:
        right = [(i, i + shift) for i in range(count - shift)]
        left = [(i + shift, i) for i in range(count - shift)]
        last = 2 * shift >= count
        if last:
            got_sum = lax.ppermute(fwd_sum, "seq", right)
            got_cot = lax.ppermute(bwd_sum, "seq", left)
        else:
            got_map, got_sum = lax.ppermute((fwd_map, fwd_sum), "seq", right)
            got_bmap, got_cot = lax.ppermute((bwd_map, bwd_sum), "seq", left)
        fwd_sum = mm("hij,hjk->hik", fwd_map, got_sum) + fwd_sum
        bwd_sum = mm("hji,hjk->hik", bwd_map, got_cot) + bwd_sum
        if not last:
            fwd_map = mm("hij,hjk->hik", fwd_map, got_map)
            bwd_map = mm("hij,hjk->hik", got_bmap, bwd_map)
        shift *= 2
    state_in = lax.ppermute(fwd_sum, "seq", [(i, i + 1) for i in range(count - 1)])
    end_cot = lax.ppermute(bwd_sum, "seq", [(i + 1, i) for i in range(count - 1)])
    return state_in, end_cot


def local(queries, reflect_keys, write_values, out_cotangent):
    tok_count, heads_here, head_size = queries.shape
    rows = 2 * tok_count
    q_raw = queries.astype(jnp.float32).transpose(1, 0, 2)
    cot = out_cotangent.astype(jnp.float32).transpose(1, 0, 2)
    k_raw = reflect_keys.astype(jnp.float32).reshape(rows, heads_here, head_size).transpose(1, 0, 2)
    vals = write_values.astype(jnp.float32).reshape(rows, heads_here, head_size).transpose(1, 0, 2)
    qn, q_scale = unit_rows(q_raw)
    kn, k_scale = unit_rows(k_raw)

    inverse = tri_inverse(kn)
    proj = mm("hij,hjd->hid", inverse, kn)
    upd_v = mm("hij,hjd->hid", inverse, vals)
    tok_ids = lax.broadcasted_iota(jnp.int32, (tok_count, rows), 0)
    sub_ids = lax.broadcasted_iota(jnp.int32, (tok_count, rows), 1)
    visible = sub_ids <= 2 * tok_ids + 1
    scores = jnp.where(visible, 2.0 * mm("hid,hjd->hij", qn, kn), 0.0)
    read_map = qn - mm("hij,hjd->hid", scores, proj)
    own_out = mm("hij,hjd->hid", scores, upd_v)
    eye = jnp.eye(head_size, dtype=jnp.float32)
    transition = eye - 2.0 * mm("hjd,hjw->hdw", kn, proj)
    offset = 2.0 * mm("hjd,hjw->hdw", kn, upd_v)
    local_cot = mm("hld,hlw->hdw", read_map, cot)

    state_in, end_cot = scan_seq(transition, offset, local_cot)

    produced = mm("hld,hdw->hlw", read_map, state_in) + own_out
    updates = upd_v - mm("hjd,hdw->hjw", proj, state_in)
    d_upd = mm("hij,hiw->hjw", scores, cot) + 2.0 * mm("hjd,hdw->hjw", kn, end_cot)
    d_w = mm("hij,hiw->hjw", inverse, d_upd)
    touch = jnp.where(visible, mm("hiw,hjw->hij", cot, updates), 0.0)
    d_qn = mm("hiw,hdw->hid", cot, state_in) + 2.0 * mm("hij,hjd->hid", touch, kn)
    gram_cot = jnp.where(strict_lower(rows, rows), -2.0 * mm("hiw,hjw->hij", d_w, updates), 0.0)
    d_kn = (
        2.0 * mm("hij,hid->hjd", touch, qn)
        + 2.0 * mm("hjw,hdw->hjd", updates, end_cot)
        - mm("hjw,hdw->hjd", d_w, state_in)
        + mm("hij,hjd->hid", gram_cot, kn)
        + mm("hji,hjd->hid", gram_cot, kn)
    )
    d_q = q_scale * (d_qn - jnp.sum(qn * d_qn, axis=-1, keepdims=True) * qn)
    d_k = k_scale * (d_kn - jnp.sum(kn * d_kn, axis=-1, keepdims=True) * kn)

    def token_major(tensor):
        return tensor.transpose(1, 0, 2).astype(jnp.bfloat16)

    def pair_major(tensor):
        return (
            tensor.reshape(heads_here, tok_count, 2, head_size)
            .transpose(1, 2, 0, 3)
            .astype(jnp.bfloat16)
        )

    return (token_major(produced), token_major(d_q), pair_major(d_k), pair_major(d_w))


def solution(mesh):
    in_specs = (
        P(("groups", "seq"), "head", None),
        P(("groups", "seq"), None, "head", None),
        P(("groups", "seq"), None, "head", None),
        P(("groups", "seq"), "head", None),
    )
    out_specs = (
        P(("groups", "seq"), "head", None),
        P(("groups", "seq"), "head", None),
        P(("groups", "seq"), None, "head", None),
        P(("groups", "seq"), None, "head", None),
    )
    return jax.shard_map(local, mesh=mesh, in_specs=in_specs, out_specs=out_specs, check_vma=False)
```

```python
import jax
import jax.numpy as jnp
from jax import lax
from jax.sharding import PartitionSpec as P

highest = lax.Precision.HIGHEST
LEAF = 16


def mm(spec, *operands):
    return jnp.einsum(spec, *operands, precision=highest)


def unit_rows(tensor):
    scale = lax.rsqrt(jnp.sum(tensor * tensor, axis=-1, keepdims=True) + 1e-06)
    return tensor * scale, scale


def strict_lower(rows, cols):
    return lax.broadcasted_iota(jnp.int32, (rows, cols), 0) > lax.broadcasted_iota(
        jnp.int32, (rows, cols), 1
    )


def tri_inverse(keys):
    heads, rows, size = keys.shape
    leaves = rows // LEAF
    leaf_keys = keys.reshape(heads, leaves, LEAF, size)
    gram = mm("hpid,hpjd->hpij", leaf_keys, leaf_keys)
    power = jnp.where(strict_lower(LEAF, LEAF), -2.0 * gram, 0.0)
    eye = jnp.eye(LEAF, dtype=jnp.float32)
    inverse = eye + power
    reach = 2
    while reach < LEAF:
        power = mm("hpij,hpjk->hpik", power, power)
        inverse = inverse + mm("hpij,hpjk->hpik", inverse, power)
        reach *= 2
    span = LEAF
    while span < rows:
        pairs = rows // (2 * span)
        blocks = inverse.reshape(heads, pairs, 2, span, span)
        upper_inv = blocks[:, :, 0]
        lower_inv = blocks[:, :, 1]
        halves = keys.reshape(heads, pairs, 2, span, size)
        link = 2.0 * mm("hpid,hpjd->hpij", halves[:, :, 1], halves[:, :, 0])
        corner = -mm("hpij,hpjk->hpik", lower_inv, mm("hpij,hpjk->hpik", link, upper_inv))
        top = jnp.concatenate([upper_inv, jnp.zeros_like(upper_inv)], axis=3)
        bottom = jnp.concatenate([corner, lower_inv], axis=3)
        inverse = jnp.concatenate([top, bottom], axis=2)
        span *= 2
    return inverse.reshape(heads, rows, rows)


def scan_seq(transition, offset, local_cot):
    count = lax.axis_size("seq")
    if count == 1:
        zero = jnp.zeros_like(offset)
        return zero, zero
    fwd_map, fwd_sum = transition, offset
    bwd_map, bwd_sum = transition, local_cot
    ex_map = ex_sum = bx_map = bx_sum = None
    shift = 1
    while shift < count:
        right = [(i, i + shift) for i in range(count - shift)]
        left = [(i + shift, i) for i in range(count - shift)]
        last = 2 * shift >= count
        if last:
            got_sum = lax.ppermute(fwd_sum, "seq", right)
            got_cot = lax.ppermute(bwd_sum, "seq", left)
        else:
            got_map, got_sum = lax.ppermute(jnp.stack([fwd_map, fwd_sum]), "seq", right)
            got_bmap, got_cot = lax.ppermute(jnp.stack([bwd_map, bwd_sum]), "seq", left)
        if ex_map is None:
            ex_map, ex_sum = (None if last else got_map), got_sum
            bx_map, bx_sum = (None if last else got_bmap), got_cot
        else:
            ex_sum = mm("hij,hjk->hik", ex_map, got_sum) + ex_sum
            bx_sum = bx_sum + mm("hji,hjk->hik", bx_map, got_cot)
            if not last:
                ex_map = mm("hij,hjk->hik", ex_map, got_map)
                bx_map = mm("hij,hjk->hik", got_bmap, bx_map)
        if not last:
            fwd_sum = mm("hij,hjk->hik", fwd_map, got_sum) + fwd_sum
            bwd_sum = bwd_sum + mm("hji,hjk->hik", bwd_map, got_cot)
            fwd_map = mm("hij,hjk->hik", fwd_map, got_map)
            bwd_map = mm("hij,hjk->hik", got_bmap, bwd_map)
        shift *= 2
    return ex_sum, bx_sum


def local(queries, reflect_keys, write_values, out_cotangent):
    tok_count, heads_here, head_size = queries.shape
    rows = 2 * tok_count
    q_raw = queries.astype(jnp.float32).transpose(1, 0, 2)
    cot = out_cotangent.astype(jnp.float32).transpose(1, 0, 2)
    k_raw = reflect_keys.astype(jnp.float32).reshape(rows, heads_here, head_size).transpose(1, 0, 2)
    vals = write_values.astype(jnp.float32).reshape(rows, heads_here, head_size).transpose(1, 0, 2)
    qn, q_scale = unit_rows(q_raw)
    kn, k_scale = unit_rows(k_raw)

    inverse = tri_inverse(kn)
    proj = mm("hij,hjd->hid", inverse, kn)
    upd_v = mm("hij,hjd->hid", inverse, vals)
    tok_ids = lax.broadcasted_iota(jnp.int32, (tok_count, rows), 0)
    sub_ids = lax.broadcasted_iota(jnp.int32, (tok_count, rows), 1)
    visible = sub_ids <= 2 * tok_ids + 1
    scores = jnp.where(visible, 2.0 * mm("hid,hjd->hij", qn, kn), 0.0)
    read_map = qn - mm("hij,hjd->hid", scores, proj)
    own_out = mm("hij,hjd->hid", scores, upd_v)
    eye = jnp.eye(head_size, dtype=jnp.float32)
    transition = eye - 2.0 * mm("hjd,hjw->hdw", kn, proj)
    offset = 2.0 * mm("hjd,hjw->hdw", kn, upd_v)
    local_cot = mm("hld,hlw->hdw", read_map, cot)

    state_in, end_cot = scan_seq(transition, offset, local_cot)

    produced = mm("hld,hdw->hlw", read_map, state_in) + own_out
    updates = upd_v - mm("hjd,hdw->hjw", proj, state_in)
    d_upd = mm("hij,hiw->hjw", scores, cot) + 2.0 * mm("hjd,hdw->hjw", kn, end_cot)
    d_w = mm("hij,hiw->hjw", inverse, d_upd)
    touch = jnp.where(visible, mm("hiw,hjw->hij", cot, updates), 0.0)
    d_qn = mm("hiw,hdw->hid", cot, state_in) + 2.0 * mm("hij,hjd->hid", touch, kn)
    gram_cot = jnp.where(strict_lower(rows, rows), -2.0 * mm("hiw,hjw->hij", d_w, updates), 0.0)
    d_kn = (
        2.0 * mm("hij,hid->hjd", touch, qn)
        + 2.0 * mm("hjw,hdw->hjd", updates, end_cot)
        - mm("hjw,hdw->hjd", d_w, state_in)
        + mm("hij,hjd->hid", gram_cot, kn)
        + mm("hji,hjd->hid", gram_cot, kn)
    )
    d_q = q_scale * (d_qn - jnp.sum(qn * d_qn, axis=-1, keepdims=True) * qn)
    d_k = k_scale * (d_kn - jnp.sum(kn * d_kn, axis=-1, keepdims=True) * kn)

    def token_major(tensor):
        return tensor.transpose(1, 0, 2).astype(jnp.bfloat16)

    def pair_major(tensor):
        return (
            tensor.reshape(heads_here, tok_count, 2, head_size)
            .transpose(1, 2, 0, 3)
            .astype(jnp.bfloat16)
        )

    return (token_major(produced), token_major(d_q), pair_major(d_k), pair_major(d_w))


def solution(mesh):
    in_specs = (
        P(("groups", "seq"), "head", None),
        P(("groups", "seq"), None, "head", None),
        P(("groups", "seq"), None, "head", None),
        P(("groups", "seq"), "head", None),
    )
    out_specs = (
        P(("groups", "seq"), "head", None),
        P(("groups", "seq"), "head", None),
        P(("groups", "seq"), None, "head", None),
        P(("groups", "seq"), None, "head", None),
    )
    return jax.shard_map(local, mesh=mesh, in_specs=in_specs, out_specs=out_specs, check_vma=False)
```

```python
import jax
import jax.numpy as jnp
from jax import lax
from jax.experimental import pallas as pl
from jax.sharding import PartitionSpec as P

highest = lax.Precision.HIGHEST
LEAF = 16


def mm(spec, *operands):
    return jnp.einsum(spec, *operands, precision=highest)


def unit_rows(tensor):
    scale = lax.rsqrt(jnp.sum(tensor * tensor, axis=-1, keepdims=True) + 1e-06)
    return tensor * scale, scale


def strict_lower(rows, cols):
    return lax.broadcasted_iota(jnp.int32, (rows, cols), 0) > lax.broadcasted_iota(
        jnp.int32, (rows, cols), 1
    )


def tri_inverse(keys):
    heads, rows, size = keys.shape
    leaves = rows // LEAF
    leaf_keys = keys.reshape(heads, leaves, LEAF, size)
    gram = mm("hpid,hpjd->hpij", leaf_keys, leaf_keys)
    power = jnp.where(strict_lower(LEAF, LEAF), -2.0 * gram, 0.0)
    eye = jnp.eye(LEAF, dtype=jnp.float32)
    inverse = eye + power
    reach = 2
    while reach < LEAF:
        power = mm("hpij,hpjk->hpik", power, power)
        inverse = inverse + mm("hpij,hpjk->hpik", inverse, power)
        reach *= 2
    span = LEAF
    while span < rows:
        pairs = rows // (2 * span)
        blocks = inverse.reshape(heads, pairs, 2, span, span)
        upper_inv = blocks[:, :, 0]
        lower_inv = blocks[:, :, 1]
        halves = keys.reshape(heads, pairs, 2, span, size)
        link = 2.0 * mm("hpid,hpjd->hpij", halves[:, :, 1], halves[:, :, 0])
        corner = -mm("hpij,hpjk->hpik", lower_inv, mm("hpij,hpjk->hpik", link, upper_inv))
        top = jnp.concatenate([upper_inv, jnp.zeros_like(upper_inv)], axis=3)
        bottom = jnp.concatenate([corner, lower_inv], axis=3)
        inverse = jnp.concatenate([top, bottom], axis=2)
        span *= 2
    return inverse.reshape(heads, rows, rows)


TILE = 128


def dot(left, right, t_left=False, t_right=False):
    dims = (((0 if t_left else 1,), (1 if t_right else 0,)), ((), ()))
    return lax.dot_general(
        left, right, dims, precision=highest, preferred_element_type=jnp.float32
    )


def ids(rows, cols):
    return (
        lax.broadcasted_iota(jnp.int32, (rows, cols), 0),
        lax.broadcasted_iota(jnp.int32, (rows, cols), 1),
    )


def normed(tensor):
    scale = lax.rsqrt(jnp.sum(tensor * tensor, axis=-1, keepdims=True) + 1e-06)
    return tensor * scale, scale


def tile_inverse(link):
    row, col = ids(TILE, TILE)
    eye = jnp.where(row == col, 1.0, 0.0).astype(jnp.float32)
    power = jnp.where(row // LEAF == col // LEAF, -link, 0.0)
    inverse = eye + power
    reach = 2
    while reach < LEAF:
        power = dot(power, power)
        inverse = inverse + dot(inverse, power)
        reach *= 2
    span = LEAF
    while span < TILE:
        cross = (row // (2 * span) == col // (2 * span)) & (row // span != col // span)
        inverse = inverse - dot(inverse, dot(jnp.where(cross, link, 0.0), inverse))
        span *= 2
    return inverse


def front_kernel(q_ref, k_ref, v_ref, c_ref, inv_ref, proj_ref, updv_ref, scores_ref,
                 rmap_ref, own_ref, trans_ref, off_ref, lc_ref):
    rows = k_ref.shape[1]
    size = k_ref.shape[2]
    toks = q_ref.shape[1]
    tiles = rows // TILE
    qn, _ = normed(q_ref[0])
    kn, _ = normed(k_ref[0])
    vals = v_ref[0]
    cot = c_ref[0]
    row, col = ids(TILE, TILE)
    key_tiles = [kn[t * TILE:(t + 1) * TILE] for t in range(tiles)]
    val_tiles = [vals[t * TILE:(t + 1) * TILE] for t in range(tiles)]
    inv = {}
    for i in range(tiles):
        gram = dot(key_tiles[i], key_tiles[i], t_right=True)
        inv[i, i] = tile_inverse(jnp.where(row > col, 2.0 * gram, 0.0))
        for j in range(i - 1, -1, -1):
            acc = None
            for m in range(j, i):
                link = 2.0 * dot(key_tiles[i], key_tiles[m], t_right=True)
                term = dot(link, inv[m, j])
                acc = term if acc is None else acc + term
            inv[i, j] = -dot(inv[i, i], acc)
    zero_tile = jnp.zeros((TILE, TILE), jnp.float32)
    for i in range(tiles):
        for j in range(tiles):
            inv_ref[0, i * TILE:(i + 1) * TILE, j * TILE:(j + 1) * TILE] = inv.get((i, j), zero_tile)
        proj_i = None
        updv_i = None
        for j in range(i + 1):
            p_term = dot(inv[i, j], key_tiles[j])
            u_term = dot(inv[i, j], val_tiles[j])
            proj_i = p_term if proj_i is None else proj_i + p_term
            updv_i = u_term if updv_i is None else updv_i + u_term
        proj_ref[0, i * TILE:(i + 1) * TILE, :] = proj_i
        updv_ref[0, i * TILE:(i + 1) * TILE, :] = updv_i
    proj = proj_ref[0]
    updv = updv_ref[0]
    tok_ids, sub_ids = ids(toks, rows)
    scores = jnp.where(sub_ids <= 2 * tok_ids + 1, 2.0 * dot(qn, kn, t_right=True), 0.0)
    scores_ref[0] = scores
    rmap = qn - dot(scores, proj)
    rmap_ref[0] = rmap
    own_ref[0] = dot(scores, updv)
    er, ec = ids(size, size)
    trans_ref[0] = jnp.where(er == ec, 1.0, 0.0) - 2.0 * dot(kn, proj, t_left=True)
    off_ref[0] = 2.0 * dot(kn, updv, t_left=True)
    lc_ref[0] = dot(rmap, cot, t_left=True)


def back_kernel(q_ref, k_ref, c_ref, s0_ref, lam_ref, inv_ref, proj_ref, updv_ref, scores_ref,
                rmap_ref, own_ref, out_ref, dq_ref, dk_ref, dv_ref):
    rows = k_ref.shape[1]
    toks = q_ref.shape[1]
    qn, q_scale = normed(q_ref[0])
    kn, k_scale = normed(k_ref[0])
    cot = c_ref[0]
    state = s0_ref[0]
    lam = lam_ref[0]
    scores = scores_ref[0]
    out_ref[0] = dot(rmap_ref[0], state) + own_ref[0]
    updates = updv_ref[0] - dot(proj_ref[0], state)
    d_upd = dot(scores, cot, t_left=True) + 2.0 * dot(kn, lam)
    d_w = dot(inv_ref[0], d_upd, t_left=True)
    dv_ref[0] = d_w
    tok_ids, sub_ids = ids(toks, rows)
    touch = jnp.where(sub_ids <= 2 * tok_ids + 1, dot(cot, updates, t_right=True), 0.0)
    d_qn = dot(cot, state, t_right=True) + 2.0 * dot(touch, kn)
    dq_ref[0] = q_scale * (d_qn - jnp.sum(qn * d_qn, axis=-1, keepdims=True) * qn)
    row, col = ids(rows, rows)
    gram_cot = jnp.where(row > col, -2.0 * dot(d_w, updates, t_right=True), 0.0)
    d_kn = (
        2.0 * dot(touch, qn, t_left=True)
        + 2.0 * dot(updates, lam, t_right=True)
        - dot(d_w, state, t_right=True)
        + dot(gram_cot, kn)
        + dot(gram_cot, kn, t_left=True)
    )
    dk_ref[0] = k_scale * (d_kn - jnp.sum(kn * d_kn, axis=-1, keepdims=True) * kn)


def per_head(shape):
    return pl.BlockSpec((1,) + tuple(shape[1:]), lambda h: (h, 0, 0))


def run_heads(kernel, operands, out_shapes):
    heads = operands[0].shape[0]
    return pl.pallas_call(
        kernel,
        grid=(heads,),
        in_specs=[per_head(x.shape) for x in operands],
        out_specs=[per_head(s) for s in out_shapes],
        out_shape=[jax.ShapeDtypeStruct(s, jnp.float32) for s in out_shapes],
    )(*operands)


def chain_seq(transition, offset, local_cot):
    count = lax.axis_size("seq")
    right = [(i, i + 1) for i in range(count - 1)]
    left = [(i + 1, i) for i in range(count - 1)]
    fwd_sum, bwd_sum = offset, local_cot
    for hop in range(count - 1):
        got_sum = lax.ppermute(fwd_sum, "seq", right)
        got_cot = lax.ppermute(bwd_sum, "seq", left)
        if hop == count - 2:
            return got_sum, got_cot
        fwd_sum = mm("hij,hjk->hik", transition, got_sum) + offset
        bwd_sum = mm("hji,hjk->hik", transition, got_cot) + local_cot
    zero = jnp.zeros_like(offset)
    return zero, zero


def scan_seq(transition, offset, local_cot):
    count = lax.axis_size("seq")
    if count <= 4:
        return chain_seq(transition, offset, local_cot)
    fwd_map, fwd_sum = transition, offset
    bwd_map, bwd_sum = transition, local_cot
    ex_map = ex_sum = bx_map = bx_sum = None
    shift = 1
    while shift < count:
        right = [(i, i + shift) for i in range(count - shift)]
        left = [(i + shift, i) for i in range(count - shift)]
        last = 2 * shift >= count
        if last:
            got_sum = lax.ppermute(fwd_sum, "seq", right)
            got_cot = lax.ppermute(bwd_sum, "seq", left)
        else:
            got_map, got_sum = lax.ppermute(jnp.stack([fwd_map, fwd_sum]), "seq", right)
            got_bmap, got_cot = lax.ppermute(jnp.stack([bwd_map, bwd_sum]), "seq", left)
        if ex_map is None:
            ex_map, ex_sum = (None if last else got_map), got_sum
            bx_map, bx_sum = (None if last else got_bmap), got_cot
        else:
            ex_sum = mm("hij,hjk->hik", ex_map, got_sum) + ex_sum
            bx_sum = bx_sum + mm("hji,hjk->hik", bx_map, got_cot)
            if not last:
                ex_map = mm("hij,hjk->hik", ex_map, got_map)
                bx_map = mm("hij,hjk->hik", got_bmap, bx_map)
        if not last:
            fwd_sum = mm("hij,hjk->hik", fwd_map, got_sum) + fwd_sum
            bwd_sum = bwd_sum + mm("hji,hjk->hik", bwd_map, got_cot)
            fwd_map = mm("hij,hjk->hik", fwd_map, got_map)
            bwd_map = mm("hij,hjk->hik", got_bmap, bwd_map)
        shift *= 2
    return ex_sum, bx_sum


def local(queries, reflect_keys, write_values, out_cotangent):
    tok_count, heads_here, head_size = queries.shape
    rows = 2 * tok_count
    q_raw = queries.astype(jnp.float32).transpose(1, 0, 2)
    cot = out_cotangent.astype(jnp.float32).transpose(1, 0, 2)
    k_raw = reflect_keys.astype(jnp.float32).reshape(rows, heads_here, head_size).transpose(1, 0, 2)
    vals = write_values.astype(jnp.float32).reshape(rows, heads_here, head_size).transpose(1, 0, 2)
    h, d = heads_here, head_size
    inverse, proj, upd_v, scores, read_map, own_out, transition, offset, local_cot = run_heads(
        front_kernel,
        (q_raw, k_raw, vals, cot),
        [(h, rows, rows), (h, rows, d), (h, rows, d), (h, tok_count, rows), (h, tok_count, d),
         (h, tok_count, d), (h, d, d), (h, d, d), (h, d, d)],
    )

    state_in, end_cot = scan_seq(transition, offset, local_cot)

    produced, d_q, d_k, d_w = run_heads(
        back_kernel,
        (q_raw, k_raw, cot, state_in, end_cot, inverse, proj, upd_v, scores, read_map, own_out),
        [(h, tok_count, d), (h, tok_count, d), (h, rows, d), (h, rows, d)],
    )

    def token_major(tensor):
        return tensor.transpose(1, 0, 2).astype(jnp.bfloat16)

    def pair_major(tensor):
        return (
            tensor.reshape(heads_here, tok_count, 2, head_size)
            .transpose(1, 2, 0, 3)
            .astype(jnp.bfloat16)
        )

    return (token_major(produced), token_major(d_q), pair_major(d_k), pair_major(d_w))


def solution(mesh):
    in_specs = (
        P(("groups", "seq"), "head", None),
        P(("groups", "seq"), None, "head", None),
        P(("groups", "seq"), None, "head", None),
        P(("groups", "seq"), "head", None),
    )
    out_specs = (
        P(("groups", "seq"), "head", None),
        P(("groups", "seq"), "head", None),
        P(("groups", "seq"), None, "head", None),
        P(("groups", "seq"), None, "head", None),
    )
    return jax.shard_map(local, mesh=mesh, in_specs=in_specs, out_specs=out_specs, check_vma=False)
```

```python
import jax
import jax.numpy as jnp
from jax import lax
from jax.sharding import PartitionSpec as P

highest = lax.Precision.HIGHEST
LEAF = 16


def mm(spec, *operands):
    return jnp.einsum(spec, *operands, precision=highest)


def unit_rows(tensor):
    scale = lax.rsqrt(jnp.sum(tensor * tensor, axis=-1, keepdims=True) + 1e-06)
    return tensor * scale, scale


def strict_lower(rows, cols):
    return lax.broadcasted_iota(jnp.int32, (rows, cols), 0) > lax.broadcasted_iota(
        jnp.int32, (rows, cols), 1
    )


def tri_inverse(keys):
    heads, rows, size = keys.shape
    leaves = rows // LEAF
    leaf_keys = keys.reshape(heads, leaves, LEAF, size)
    gram = mm("hpid,hpjd->hpij", leaf_keys, leaf_keys)
    power = jnp.where(strict_lower(LEAF, LEAF), -2.0 * gram, 0.0)
    eye = jnp.eye(LEAF, dtype=jnp.float32)
    inverse = eye + power
    reach = 2
    while reach < LEAF:
        power = mm("hpij,hpjk->hpik", power, power)
        inverse = inverse + mm("hpij,hpjk->hpik", inverse, power)
        reach *= 2
    span = LEAF
    while span < rows:
        pairs = rows // (2 * span)
        blocks = inverse.reshape(heads, pairs, 2, span, span)
        upper_inv = blocks[:, :, 0]
        lower_inv = blocks[:, :, 1]
        halves = keys.reshape(heads, pairs, 2, span, size)
        link = 2.0 * mm("hpid,hpjd->hpij", halves[:, :, 1], halves[:, :, 0])
        corner = -mm("hpij,hpjk->hpik", lower_inv, mm("hpij,hpjk->hpik", link, upper_inv))
        top = jnp.concatenate([upper_inv, jnp.zeros_like(upper_inv)], axis=3)
        bottom = jnp.concatenate([corner, lower_inv], axis=3)
        inverse = jnp.concatenate([top, bottom], axis=2)
        span *= 2
    return inverse.reshape(heads, rows, rows)


def crossing_pairs(count, width, core_goes_right):
    pairs = []
    for s in range(count):
        for h in range(width):
            target = s + 1 if (h % 2 == 0) == core_goes_right else s - 1
            if 0 <= target < count:
                pairs.append((s * width + h, target * width + h))
    return pairs


def chain_seq(transition, offset, local_cot):
    count = lax.axis_size("seq")
    width = lax.axis_size("head")
    even = lax.axis_index("head") % 2 == 0
    first = crossing_pairs(count, width, True)
    second = crossing_pairs(count, width, False)
    axes = ("seq", "head")
    fwd_sum, bwd_sum = offset, local_cot
    for hop in range(count - 1):
        got_first = lax.ppermute(jnp.where(even, fwd_sum, bwd_sum), axes, first)
        got_second = lax.ppermute(jnp.where(even, bwd_sum, fwd_sum), axes, second)
        got_sum = jnp.where(even, got_first, got_second)
        got_cot = jnp.where(even, got_second, got_first)
        if hop == count - 2:
            return got_sum, got_cot
        fwd_sum = mm("hij,hjk->hik", transition, got_sum) + offset
        bwd_sum = mm("hji,hjk->hik", transition, got_cot) + local_cot
    zero = jnp.zeros_like(offset)
    return zero, zero


def scan_seq(transition, offset, local_cot):
    count = lax.axis_size("seq")
    if count <= 4:
        return chain_seq(transition, offset, local_cot)
    fwd_map, fwd_sum = transition, offset
    bwd_map, bwd_sum = transition, local_cot
    shift = 1
    while shift < count:
        right = [(i, i + shift) for i in range(count - shift)]
        left = [(i + shift, i) for i in range(count - shift)]
        last = 2 * shift >= count
        if last:
            got_sum = lax.ppermute(fwd_sum, "seq", right)
            got_cot = lax.ppermute(bwd_sum, "seq", left)
        else:
            got_map, got_sum = lax.ppermute((fwd_map, fwd_sum), "seq", right)
            got_bmap, got_cot = lax.ppermute((bwd_map, bwd_sum), "seq", left)
        fwd_sum = mm("hij,hjk->hik", fwd_map, got_sum) + fwd_sum
        bwd_sum = mm("hji,hjk->hik", bwd_map, got_cot) + bwd_sum
        if not last:
            fwd_map = mm("hij,hjk->hik", fwd_map, got_map)
            bwd_map = mm("hij,hjk->hik", got_bmap, bwd_map)
        shift *= 2
    state_in = lax.ppermute(fwd_sum, "seq", [(i, i + 1) for i in range(count - 1)])
    end_cot = lax.ppermute(bwd_sum, "seq", [(i + 1, i) for i in range(count - 1)])
    return state_in, end_cot


def local(queries, reflect_keys, write_values, out_cotangent):
    tok_count, heads_here, head_size = queries.shape
    rows = 2 * tok_count
    q_raw = queries.astype(jnp.float32).transpose(1, 0, 2)
    cot = out_cotangent.astype(jnp.float32).transpose(1, 0, 2)
    k_raw = reflect_keys.astype(jnp.float32).reshape(rows, heads_here, head_size).transpose(1, 0, 2)
    vals = write_values.astype(jnp.float32).reshape(rows, heads_here, head_size).transpose(1, 0, 2)
    qn, q_scale = unit_rows(q_raw)
    kn, k_scale = unit_rows(k_raw)

    inverse = tri_inverse(kn)
    proj = mm("hij,hjd->hid", inverse, kn)
    upd_v = mm("hij,hjd->hid", inverse, vals)
    tok_ids = lax.broadcasted_iota(jnp.int32, (tok_count, rows), 0)
    sub_ids = lax.broadcasted_iota(jnp.int32, (tok_count, rows), 1)
    visible = sub_ids <= 2 * tok_ids + 1
    scores = jnp.where(visible, 2.0 * mm("hid,hjd->hij", qn, kn), 0.0)
    read_map = qn - mm("hij,hjd->hid", scores, proj)
    own_out = mm("hij,hjd->hid", scores, upd_v)
    eye = jnp.eye(head_size, dtype=jnp.float32)
    transition = eye - 2.0 * mm("hjd,hjw->hdw", kn, proj)
    offset = 2.0 * mm("hjd,hjw->hdw", kn, upd_v)
    local_cot = mm("hld,hlw->hdw", read_map, cot)

    state_in, end_cot = scan_seq(transition, offset, local_cot)

    produced = mm("hld,hdw->hlw", read_map, state_in) + own_out
    updates = upd_v - mm("hjd,hdw->hjw", proj, state_in)
    d_upd = mm("hij,hiw->hjw", scores, cot) + 2.0 * mm("hjd,hdw->hjw", kn, end_cot)
    d_w = mm("hij,hiw->hjw", inverse, d_upd)
    touch = jnp.where(visible, mm("hiw,hjw->hij", cot, updates), 0.0)
    d_qn = mm("hiw,hdw->hid", cot, state_in) + 2.0 * mm("hij,hjd->hid", touch, kn)
    gram_cot = jnp.where(strict_lower(rows, rows), -2.0 * mm("hiw,hjw->hij", d_w, updates), 0.0)
    d_kn = (
        2.0 * mm("hij,hid->hjd", touch, qn)
        + 2.0 * mm("hjw,hdw->hjd", updates, end_cot)
        - mm("hjw,hdw->hjd", d_w, state_in)
        + mm("hij,hjd->hid", gram_cot, kn)
        + mm("hji,hjd->hid", gram_cot, kn)
    )
    d_q = q_scale * (d_qn - jnp.sum(qn * d_qn, axis=-1, keepdims=True) * qn)
    d_k = k_scale * (d_kn - jnp.sum(kn * d_kn, axis=-1, keepdims=True) * kn)

    def token_major(tensor):
        return tensor.transpose(1, 0, 2).astype(jnp.bfloat16)

    def pair_major(tensor):
        return (
            tensor.reshape(heads_here, tok_count, 2, head_size)
            .transpose(1, 2, 0, 3)
            .astype(jnp.bfloat16)
        )

    return (token_major(produced), token_major(d_q), pair_major(d_k), pair_major(d_w))


def solution(mesh):
    in_specs = (
        P(("groups", "seq"), "head", None),
        P(("groups", "seq"), None, "head", None),
        P(("groups", "seq"), None, "head", None),
        P(("groups", "seq"), "head", None),
    )
    out_specs = (
        P(("groups", "seq"), "head", None),
        P(("groups", "seq"), "head", None),
        P(("groups", "seq"), None, "head", None),
        P(("groups", "seq"), None, "head", None),
    )
    return jax.shard_map(local, mesh=mesh, in_specs=in_specs, out_specs=out_specs, check_vma=False)
```

```python
import jax
import jax.numpy as jnp
from jax import lax
from jax.sharding import PartitionSpec as P

highest = lax.Precision.HIGHEST
LEAF = 16


def mm(spec, *operands):
    return jnp.einsum(spec, *operands, precision=highest)


def unit_rows(tensor):
    scale = lax.rsqrt(jnp.sum(tensor * tensor, axis=-1, keepdims=True) + 1e-06)
    return tensor * scale, scale


def strict_lower(rows, cols):
    return lax.broadcasted_iota(jnp.int32, (rows, cols), 0) > lax.broadcasted_iota(
        jnp.int32, (rows, cols), 1
    )


def tri_inverse(keys):
    heads, rows, size = keys.shape
    leaves = rows // LEAF
    leaf_keys = keys.reshape(heads, leaves, LEAF, size)
    gram = mm("hpid,hpjd->hpij", leaf_keys, leaf_keys)
    power = jnp.where(strict_lower(LEAF, LEAF), -2.0 * gram, 0.0)
    eye = jnp.eye(LEAF, dtype=jnp.float32)
    inverse = eye + power
    reach = 2
    while reach < LEAF:
        power = mm("hpij,hpjk->hpik", power, power)
        inverse = inverse + mm("hpij,hpjk->hpik", inverse, power)
        reach *= 2
    span = LEAF
    while span < rows:
        pairs = rows // (2 * span)
        blocks = inverse.reshape(heads, pairs, 2, span, span)
        upper_inv = blocks[:, :, 0]
        lower_inv = blocks[:, :, 1]
        halves = keys.reshape(heads, pairs, 2, span, size)
        link = 2.0 * mm("hpid,hpjd->hpij", halves[:, :, 1], halves[:, :, 0])
        corner = -mm("hpij,hpjk->hpik", lower_inv, mm("hpij,hpjk->hpik", link, upper_inv))
        top = jnp.concatenate([upper_inv, jnp.zeros_like(upper_inv)], axis=3)
        bottom = jnp.concatenate([corner, lower_inv], axis=3)
        inverse = jnp.concatenate([top, bottom], axis=2)
        span *= 2
    return inverse.reshape(heads, rows, rows)


def chain_seq(transition, offset, local_cot):
    count = lax.axis_size("seq")
    here = lax.axis_index("seq")
    state_in = jnp.zeros_like(offset)
    end_cot = jnp.zeros_like(local_cot)
    fwd_sum, bwd_sum = offset, local_cot
    for hop in range(1, count):
        sender = hop - 1
        back_sender = count - hop
        payload = jnp.where(here == sender, fwd_sum, bwd_sum)
        got = lax.ppermute(payload, "seq", [(sender, hop), (back_sender, back_sender - 1)])
        state_in = jnp.where(here == hop, got, state_in)
        end_cot = jnp.where(here == back_sender - 1, got, end_cot)
        if hop < count - 1:
            fwd_sum = mm("hij,hjk->hik", transition, state_in) + offset
            bwd_sum = mm("hji,hjk->hik", transition, end_cot) + local_cot
    return state_in, end_cot


def scan_seq(transition, offset, local_cot):
    count = lax.axis_size("seq")
    if count <= 4:
        return chain_seq(transition, offset, local_cot)
    fwd_map, fwd_sum = transition, offset
    bwd_map, bwd_sum = transition, local_cot
    shift = 1
    while shift < count:
        right = [(i, i + shift) for i in range(count - shift)]
        left = [(i + shift, i) for i in range(count - shift)]
        last = 2 * shift >= count
        if last:
            got_sum = lax.ppermute(fwd_sum, "seq", right)
            got_cot = lax.ppermute(bwd_sum, "seq", left)
        else:
            got_map, got_sum = lax.ppermute((fwd_map, fwd_sum), "seq", right)
            got_bmap, got_cot = lax.ppermute((bwd_map, bwd_sum), "seq", left)
        fwd_sum = mm("hij,hjk->hik", fwd_map, got_sum) + fwd_sum
        bwd_sum = mm("hji,hjk->hik", bwd_map, got_cot) + bwd_sum
        if not last:
            fwd_map = mm("hij,hjk->hik", fwd_map, got_map)
            bwd_map = mm("hij,hjk->hik", got_bmap, bwd_map)
        shift *= 2
    state_in = lax.ppermute(fwd_sum, "seq", [(i, i + 1) for i in range(count - 1)])
    end_cot = lax.ppermute(bwd_sum, "seq", [(i + 1, i) for i in range(count - 1)])
    return state_in, end_cot


def local(queries, reflect_keys, write_values, out_cotangent):
    tok_count, heads_here, head_size = queries.shape
    rows = 2 * tok_count
    q_raw = queries.astype(jnp.float32).transpose(1, 0, 2)
    cot = out_cotangent.astype(jnp.float32).transpose(1, 0, 2)
    k_raw = reflect_keys.astype(jnp.float32).reshape(rows, heads_here, head_size).transpose(1, 0, 2)
    vals = write_values.astype(jnp.float32).reshape(rows, heads_here, head_size).transpose(1, 0, 2)
    qn, q_scale = unit_rows(q_raw)
    kn, k_scale = unit_rows(k_raw)

    inverse = tri_inverse(kn)
    proj = mm("hij,hjd->hid", inverse, kn)
    upd_v = mm("hij,hjd->hid", inverse, vals)
    tok_ids = lax.broadcasted_iota(jnp.int32, (tok_count, rows), 0)
    sub_ids = lax.broadcasted_iota(jnp.int32, (tok_count, rows), 1)
    visible = sub_ids <= 2 * tok_ids + 1
    scores = jnp.where(visible, 2.0 * mm("hid,hjd->hij", qn, kn), 0.0)
    read_map = qn - mm("hij,hjd->hid", scores, proj)
    own_out = mm("hij,hjd->hid", scores, upd_v)
    eye = jnp.eye(head_size, dtype=jnp.float32)
    transition = eye - 2.0 * mm("hjd,hjw->hdw", kn, proj)
    offset = 2.0 * mm("hjd,hjw->hdw", kn, upd_v)
    local_cot = mm("hld,hlw->hdw", read_map, cot)

    state_in, end_cot = scan_seq(transition, offset, local_cot)

    produced = mm("hld,hdw->hlw", read_map, state_in) + own_out
    updates = upd_v - mm("hjd,hdw->hjw", proj, state_in)
    d_upd = mm("hij,hiw->hjw", scores, cot) + 2.0 * mm("hjd,hdw->hjw", kn, end_cot)
    d_w = mm("hij,hiw->hjw", inverse, d_upd)
    touch = jnp.where(visible, mm("hiw,hjw->hij", cot, updates), 0.0)
    d_qn = mm("hiw,hdw->hid", cot, state_in) + 2.0 * mm("hij,hjd->hid", touch, kn)
    gram_cot = jnp.where(strict_lower(rows, rows), -2.0 * mm("hiw,hjw->hij", d_w, updates), 0.0)
    d_kn = (
        2.0 * mm("hij,hid->hjd", touch, qn)
        + 2.0 * mm("hjw,hdw->hjd", updates, end_cot)
        - mm("hjw,hdw->hjd", d_w, state_in)
        + mm("hij,hjd->hid", gram_cot, kn)
        + mm("hji,hjd->hid", gram_cot, kn)
    )
    d_q = q_scale * (d_qn - jnp.sum(qn * d_qn, axis=-1, keepdims=True) * qn)
    d_k = k_scale * (d_kn - jnp.sum(kn * d_kn, axis=-1, keepdims=True) * kn)

    def token_major(tensor):
        return tensor.transpose(1, 0, 2).astype(jnp.bfloat16)

    def pair_major(tensor):
        return (
            tensor.reshape(heads_here, tok_count, 2, head_size)
            .transpose(1, 2, 0, 3)
            .astype(jnp.bfloat16)
        )

    return (token_major(produced), token_major(d_q), pair_major(d_k), pair_major(d_w))


def solution(mesh):
    in_specs = (
        P(("groups", "seq"), "head", None),
        P(("groups", "seq"), None, "head", None),
        P(("groups", "seq"), None, "head", None),
        P(("groups", "seq"), "head", None),
    )
    out_specs = (
        P(("groups", "seq"), "head", None),
        P(("groups", "seq"), "head", None),
        P(("groups", "seq"), None, "head", None),
        P(("groups", "seq"), None, "head", None),
    )
    return jax.shard_map(local, mesh=mesh, in_specs=in_specs, out_specs=out_specs, check_vma=False)
```

```python
import jax
import jax.numpy as jnp
from jax import lax
from jax.sharding import PartitionSpec as P

highest = lax.Precision.HIGHEST
LEAF = 16


def mm(spec, *operands):
    return jnp.einsum(spec, *operands, precision=highest)


def unit_rows(tensor):
    scale = lax.rsqrt(jnp.sum(tensor * tensor, axis=-1, keepdims=True) + 1e-06)
    return tensor * scale, scale


def strict_lower(rows, cols):
    return lax.broadcasted_iota(jnp.int32, (rows, cols), 0) > lax.broadcasted_iota(
        jnp.int32, (rows, cols), 1
    )


def tri_inverse(keys):
    heads, rows, size = keys.shape
    leaves = rows // LEAF
    leaf_keys = keys.reshape(heads, leaves, LEAF, size)
    gram = mm("hpid,hpjd->hpij", leaf_keys, leaf_keys)
    power = jnp.where(strict_lower(LEAF, LEAF), -2.0 * gram, 0.0)
    eye = jnp.eye(LEAF, dtype=jnp.float32)
    inverse = eye + power
    reach = 2
    while reach < LEAF:
        power = mm("hpij,hpjk->hpik", power, power)
        inverse = inverse + mm("hpij,hpjk->hpik", inverse, power)
        reach *= 2
    span = LEAF
    while span < rows:
        pairs = rows // (2 * span)
        blocks = inverse.reshape(heads, pairs, 2, span, span)
        upper_inv = blocks[:, :, 0]
        lower_inv = blocks[:, :, 1]
        halves = keys.reshape(heads, pairs, 2, span, size)
        link = 2.0 * mm("hpid,hpjd->hpij", halves[:, :, 1], halves[:, :, 0])
        corner = -mm("hpij,hpjk->hpik", lower_inv, mm("hpij,hpjk->hpik", link, upper_inv))
        top = jnp.concatenate([upper_inv, jnp.zeros_like(upper_inv)], axis=3)
        bottom = jnp.concatenate([corner, lower_inv], axis=3)
        inverse = jnp.concatenate([top, bottom], axis=2)
        span *= 2
    return inverse.reshape(heads, rows, rows)


def sliced_permute(tensor, pairs):
    heads = tensor.shape[0]
    parts = [lax.ppermute(tensor[h:h + 1], "seq", pairs) for h in range(heads)]
    return jnp.concatenate(parts, axis=0)


def chain_seq(transition, offset, local_cot):
    count = lax.axis_size("seq")
    right = [(i, i + 1) for i in range(count - 1)]
    left = [(i + 1, i) for i in range(count - 1)]
    fwd_sum, bwd_sum = offset, local_cot
    for hop in range(count - 1):
        got_sum = sliced_permute(fwd_sum, right)
        got_cot = sliced_permute(bwd_sum, left)
        if hop == count - 2:
            return got_sum, got_cot
        fwd_sum = mm("hij,hjk->hik", transition, got_sum) + offset
        bwd_sum = mm("hji,hjk->hik", transition, got_cot) + local_cot
    zero = jnp.zeros_like(offset)
    return zero, zero


def scan_seq(transition, offset, local_cot):
    count = lax.axis_size("seq")
    if count <= 4:
        return chain_seq(transition, offset, local_cot)
    fwd_map, fwd_sum = transition, offset
    bwd_map, bwd_sum = transition, local_cot
    shift = 1
    while shift < count:
        right = [(i, i + shift) for i in range(count - shift)]
        left = [(i + shift, i) for i in range(count - shift)]
        last = 2 * shift >= count
        if last:
            got_sum = lax.ppermute(fwd_sum, "seq", right)
            got_cot = lax.ppermute(bwd_sum, "seq", left)
        else:
            got_map, got_sum = lax.ppermute((fwd_map, fwd_sum), "seq", right)
            got_bmap, got_cot = lax.ppermute((bwd_map, bwd_sum), "seq", left)
        fwd_sum = mm("hij,hjk->hik", fwd_map, got_sum) + fwd_sum
        bwd_sum = mm("hji,hjk->hik", bwd_map, got_cot) + bwd_sum
        if not last:
            fwd_map = mm("hij,hjk->hik", fwd_map, got_map)
            bwd_map = mm("hij,hjk->hik", got_bmap, bwd_map)
        shift *= 2
    state_in = lax.ppermute(fwd_sum, "seq", [(i, i + 1) for i in range(count - 1)])
    end_cot = lax.ppermute(bwd_sum, "seq", [(i + 1, i) for i in range(count - 1)])
    return state_in, end_cot


def local(queries, reflect_keys, write_values, out_cotangent):
    tok_count, heads_here, head_size = queries.shape
    rows = 2 * tok_count
    q_raw = queries.astype(jnp.float32).transpose(1, 0, 2)
    cot = out_cotangent.astype(jnp.float32).transpose(1, 0, 2)
    k_raw = reflect_keys.astype(jnp.float32).reshape(rows, heads_here, head_size).transpose(1, 0, 2)
    vals = write_values.astype(jnp.float32).reshape(rows, heads_here, head_size).transpose(1, 0, 2)
    qn, q_scale = unit_rows(q_raw)
    kn, k_scale = unit_rows(k_raw)

    inverse = tri_inverse(kn)
    proj = mm("hij,hjd->hid", inverse, kn)
    upd_v = mm("hij,hjd->hid", inverse, vals)
    tok_ids = lax.broadcasted_iota(jnp.int32, (tok_count, rows), 0)
    sub_ids = lax.broadcasted_iota(jnp.int32, (tok_count, rows), 1)
    visible = sub_ids <= 2 * tok_ids + 1
    scores = jnp.where(visible, 2.0 * mm("hid,hjd->hij", qn, kn), 0.0)
    read_map = qn - mm("hij,hjd->hid", scores, proj)
    own_out = mm("hij,hjd->hid", scores, upd_v)
    eye = jnp.eye(head_size, dtype=jnp.float32)
    transition = eye - 2.0 * mm("hjd,hjw->hdw", kn, proj)
    offset = 2.0 * mm("hjd,hjw->hdw", kn, upd_v)
    local_cot = mm("hld,hlw->hdw", read_map, cot)

    state_in, end_cot = scan_seq(transition, offset, local_cot)

    produced = mm("hld,hdw->hlw", read_map, state_in) + own_out
    updates = upd_v - mm("hjd,hdw->hjw", proj, state_in)
    d_upd = mm("hij,hiw->hjw", scores, cot) + 2.0 * mm("hjd,hdw->hjw", kn, end_cot)
    d_w = mm("hij,hiw->hjw", inverse, d_upd)
    touch = jnp.where(visible, mm("hiw,hjw->hij", cot, updates), 0.0)
    d_qn = mm("hiw,hdw->hid", cot, state_in) + 2.0 * mm("hij,hjd->hid", touch, kn)
    gram_cot = jnp.where(strict_lower(rows, rows), -2.0 * mm("hiw,hjw->hij", d_w, updates), 0.0)
    d_kn = (
        2.0 * mm("hij,hid->hjd", touch, qn)
        + 2.0 * mm("hjw,hdw->hjd", updates, end_cot)
        - mm("hjw,hdw->hjd", d_w, state_in)
        + mm("hij,hjd->hid", gram_cot, kn)
        + mm("hji,hjd->hid", gram_cot, kn)
    )
    d_q = q_scale * (d_qn - jnp.sum(qn * d_qn, axis=-1, keepdims=True) * qn)
    d_k = k_scale * (d_kn - jnp.sum(kn * d_kn, axis=-1, keepdims=True) * kn)

    def token_major(tensor):
        return tensor.transpose(1, 0, 2).astype(jnp.bfloat16)

    def pair_major(tensor):
        return (
            tensor.reshape(heads_here, tok_count, 2, head_size)
            .transpose(1, 2, 0, 3)
            .astype(jnp.bfloat16)
        )

    return (token_major(produced), token_major(d_q), pair_major(d_k), pair_major(d_w))


def solution(mesh):
    in_specs = (
        P(("groups", "seq"), "head", None),
        P(("groups", "seq"), None, "head", None),
        P(("groups", "seq"), None, "head", None),
        P(("groups", "seq"), "head", None),
    )
    out_specs = (
        P(("groups", "seq"), "head", None),
        P(("groups", "seq"), "head", None),
        P(("groups", "seq"), None, "head", None),
        P(("groups", "seq"), None, "head", None),
    )
    return jax.shard_map(local, mesh=mesh, in_specs=in_specs, out_specs=out_specs, check_vma=False)
```

```python
import jax
import jax.numpy as jnp
from jax import lax
from jax.sharding import PartitionSpec as P

highest = lax.Precision.HIGHEST
LEAF = 16


def mm(spec, *operands):
    return jnp.einsum(spec, *operands, precision=highest)


def mh(spec, *operands):
    return jnp.einsum(spec, *operands, precision=lax.Precision.HIGH)


def unit_rows(tensor):
    scale = lax.rsqrt(jnp.sum(tensor * tensor, axis=-1, keepdims=True) + 1e-06)
    return tensor * scale, scale


def strict_lower(rows, cols):
    return lax.broadcasted_iota(jnp.int32, (rows, cols), 0) > lax.broadcasted_iota(
        jnp.int32, (rows, cols), 1
    )


def tri_inverse(keys):
    heads, rows, size = keys.shape
    leaves = rows // LEAF
    leaf_keys = keys.reshape(heads, leaves, LEAF, size)
    gram = mm("hpid,hpjd->hpij", leaf_keys, leaf_keys)
    power = jnp.where(strict_lower(LEAF, LEAF), -2.0 * gram, 0.0)
    eye = jnp.eye(LEAF, dtype=jnp.float32)
    inverse = eye + power
    reach = 2
    while reach < LEAF:
        power = mm("hpij,hpjk->hpik", power, power)
        inverse = inverse + mm("hpij,hpjk->hpik", inverse, power)
        reach *= 2
    span = LEAF
    while span < rows:
        pairs = rows // (2 * span)
        blocks = inverse.reshape(heads, pairs, 2, span, span)
        upper_inv = blocks[:, :, 0]
        lower_inv = blocks[:, :, 1]
        halves = keys.reshape(heads, pairs, 2, span, size)
        link = 2.0 * mm("hpid,hpjd->hpij", halves[:, :, 1], halves[:, :, 0])
        corner = -mm("hpij,hpjk->hpik", lower_inv, mm("hpij,hpjk->hpik", link, upper_inv))
        top = jnp.concatenate([upper_inv, jnp.zeros_like(upper_inv)], axis=3)
        bottom = jnp.concatenate([corner, lower_inv], axis=3)
        inverse = jnp.concatenate([top, bottom], axis=2)
        span *= 2
    return inverse.reshape(heads, rows, rows)


def chain_seq(transition, offset, local_cot):
    count = lax.axis_size("seq")
    right = [(i, i + 1) for i in range(count - 1)]
    left = [(i + 1, i) for i in range(count - 1)]
    fwd_sum, bwd_sum = offset, local_cot
    for hop in range(count - 1):
        got_sum = lax.ppermute(fwd_sum, "seq", right)
        got_cot = lax.ppermute(bwd_sum, "seq", left)
        if hop == count - 2:
            return got_sum, got_cot
        fwd_sum = mm("hij,hjk->hik", transition, got_sum) + offset
        bwd_sum = mm("hji,hjk->hik", transition, got_cot) + local_cot
    zero = jnp.zeros_like(offset)
    return zero, zero


def scan_seq(transition, offset, local_cot):
    count = lax.axis_size("seq")
    if count <= 4:
        return chain_seq(transition, offset, local_cot)
    fwd_map, fwd_sum = transition, offset
    bwd_map, bwd_sum = transition, local_cot
    shift = 1
    while shift < count:
        right = [(i, i + shift) for i in range(count - shift)]
        left = [(i + shift, i) for i in range(count - shift)]
        last = 2 * shift >= count
        if last:
            got_sum = lax.ppermute(fwd_sum, "seq", right)
            got_cot = lax.ppermute(bwd_sum, "seq", left)
        else:
            got_map, got_sum = lax.ppermute((fwd_map, fwd_sum), "seq", right)
            got_bmap, got_cot = lax.ppermute((bwd_map, bwd_sum), "seq", left)
        fwd_sum = mm("hij,hjk->hik", fwd_map, got_sum) + fwd_sum
        bwd_sum = mm("hji,hjk->hik", bwd_map, got_cot) + bwd_sum
        if not last:
            fwd_map = mm("hij,hjk->hik", fwd_map, got_map)
            bwd_map = mm("hij,hjk->hik", got_bmap, bwd_map)
        shift *= 2
    state_in = lax.ppermute(fwd_sum, "seq", [(i, i + 1) for i in range(count - 1)])
    end_cot = lax.ppermute(bwd_sum, "seq", [(i + 1, i) for i in range(count - 1)])
    return state_in, end_cot


def local(queries, reflect_keys, write_values, out_cotangent):
    tok_count, heads_here, head_size = queries.shape
    rows = 2 * tok_count
    q_raw = queries.astype(jnp.float32).transpose(1, 0, 2)
    cot = out_cotangent.astype(jnp.float32).transpose(1, 0, 2)
    k_raw = reflect_keys.astype(jnp.float32).reshape(rows, heads_here, head_size).transpose(1, 0, 2)
    vals = write_values.astype(jnp.float32).reshape(rows, heads_here, head_size).transpose(1, 0, 2)
    qn, q_scale = unit_rows(q_raw)
    kn, k_scale = unit_rows(k_raw)

    inverse = tri_inverse(kn)
    proj = mh("hij,hjd->hid", inverse, kn)
    upd_v = mh("hij,hjd->hid", inverse, vals)
    tok_ids = lax.broadcasted_iota(jnp.int32, (tok_count, rows), 0)
    sub_ids = lax.broadcasted_iota(jnp.int32, (tok_count, rows), 1)
    visible = sub_ids <= 2 * tok_ids + 1
    scores = jnp.where(visible, 2.0 * mh("hid,hjd->hij", qn, kn), 0.0)
    read_map = qn - mh("hij,hjd->hid", scores, proj)
    own_out = mh("hij,hjd->hid", scores, upd_v)
    eye = jnp.eye(head_size, dtype=jnp.float32)
    transition = eye - 2.0 * mh("hjd,hjw->hdw", kn, proj)
    offset = 2.0 * mh("hjd,hjw->hdw", kn, upd_v)
    local_cot = mh("hld,hlw->hdw", read_map, cot)

    state_in, end_cot = scan_seq(transition, offset, local_cot)

    produced = mh("hld,hdw->hlw", read_map, state_in) + own_out
    updates = upd_v - mh("hjd,hdw->hjw", proj, state_in)
    d_upd = mh("hij,hiw->hjw", scores, cot) + 2.0 * mh("hjd,hdw->hjw", kn, end_cot)
    d_w = mh("hij,hiw->hjw", inverse, d_upd)
    touch = jnp.where(visible, mh("hiw,hjw->hij", cot, updates), 0.0)
    d_qn = mh("hiw,hdw->hid", cot, state_in) + 2.0 * mh("hij,hjd->hid", touch, kn)
    gram_cot = jnp.where(strict_lower(rows, rows), -2.0 * mh("hiw,hjw->hij", d_w, updates), 0.0)
    d_kn = (
        2.0 * mh("hij,hid->hjd", touch, qn)
        + 2.0 * mh("hjw,hdw->hjd", updates, end_cot)
        - mh("hjw,hdw->hjd", d_w, state_in)
        + mh("hij,hjd->hid", gram_cot, kn)
        + mh("hji,hjd->hid", gram_cot, kn)
    )
    d_q = q_scale * (d_qn - jnp.sum(qn * d_qn, axis=-1, keepdims=True) * qn)
    d_k = k_scale * (d_kn - jnp.sum(kn * d_kn, axis=-1, keepdims=True) * kn)

    def token_major(tensor):
        return tensor.transpose(1, 0, 2).astype(jnp.bfloat16)

    def pair_major(tensor):
        return (
            tensor.reshape(heads_here, tok_count, 2, head_size)
            .transpose(1, 2, 0, 3)
            .astype(jnp.bfloat16)
        )

    return (token_major(produced), token_major(d_q), pair_major(d_k), pair_major(d_w))


def solution(mesh):
    in_specs = (
        P(("groups", "seq"), "head", None),
        P(("groups", "seq"), None, "head", None),
        P(("groups", "seq"), None, "head", None),
        P(("groups", "seq"), "head", None),
    )
    out_specs = (
        P(("groups", "seq"), "head", None),
        P(("groups", "seq"), "head", None),
        P(("groups", "seq"), None, "head", None),
        P(("groups", "seq"), None, "head", None),
    )
    return jax.shard_map(local, mesh=mesh, in_specs=in_specs, out_specs=out_specs, check_vma=False)
```

```python
import jax
import jax.numpy as jnp
from jax import lax
from jax.sharding import PartitionSpec as P

highest = lax.Precision.HIGHEST
LEAF = 16


def mm(spec, *operands):
    return jnp.einsum(spec, *operands, precision=highest)


def mh(spec, *operands):
    return jnp.einsum(spec, *operands, precision=lax.Precision.HIGH)


def unit_rows(tensor):
    scale = lax.rsqrt(jnp.sum(tensor * tensor, axis=-1, keepdims=True) + 1e-06)
    return tensor * scale, scale


def strict_lower(rows, cols):
    return lax.broadcasted_iota(jnp.int32, (rows, cols), 0) > lax.broadcasted_iota(
        jnp.int32, (rows, cols), 1
    )


def tri_inverse(keys):
    heads, rows, size = keys.shape
    leaves = rows // LEAF
    leaf_keys = keys.reshape(heads, leaves, LEAF, size)
    gram = mm("hpid,hpjd->hpij", leaf_keys, leaf_keys)
    power = jnp.where(strict_lower(LEAF, LEAF), -2.0 * gram, 0.0)
    eye = jnp.eye(LEAF, dtype=jnp.float32)
    inverse = eye + power
    reach = 2
    while reach < LEAF:
        power = mm("hpij,hpjk->hpik", power, power)
        inverse = inverse + mm("hpij,hpjk->hpik", inverse, power)
        reach *= 2
    span = LEAF
    while span < rows:
        pairs = rows // (2 * span)
        blocks = inverse.reshape(heads, pairs, 2, span, span)
        upper_inv = blocks[:, :, 0]
        lower_inv = blocks[:, :, 1]
        halves = keys.reshape(heads, pairs, 2, span, size)
        link = 2.0 * mm("hpid,hpjd->hpij", halves[:, :, 1], halves[:, :, 0])
        corner = -mm("hpij,hpjk->hpik", lower_inv, mm("hpij,hpjk->hpik", link, upper_inv))
        top = jnp.concatenate([upper_inv, jnp.zeros_like(upper_inv)], axis=3)
        bottom = jnp.concatenate([corner, lower_inv], axis=3)
        inverse = jnp.concatenate([top, bottom], axis=2)
        span *= 2
    return inverse.reshape(heads, rows, rows)


def chain_seq(transition, offset, local_cot):
    count = lax.axis_size("seq")
    here = lax.axis_index("seq")
    state_in = jnp.zeros_like(offset)
    end_cot = jnp.zeros_like(local_cot)
    fwd_sum, bwd_sum = offset, local_cot
    for hop in range(1, count):
        sender = hop - 1
        back_sender = count - hop
        payload = jnp.where(here == sender, fwd_sum, bwd_sum)
        got = lax.ppermute(payload, "seq", [(sender, hop), (back_sender, back_sender - 1)])
        state_in = jnp.where(here == hop, got, state_in)
        end_cot = jnp.where(here == back_sender - 1, got, end_cot)
        if hop < count - 1:
            fwd_sum = mm("hij,hjk->hik", transition, state_in) + offset
            bwd_sum = mm("hji,hjk->hik", transition, end_cot) + local_cot
    return state_in, end_cot


def scan_seq(transition, offset, local_cot):
    count = lax.axis_size("seq")
    if count <= 4:
        return chain_seq(transition, offset, local_cot)
    fwd_map, fwd_sum = transition, offset
    bwd_map, bwd_sum = transition, local_cot
    shift = 1
    while shift < count:
        right = [(i, i + shift) for i in range(count - shift)]
        left = [(i + shift, i) for i in range(count - shift)]
        last = 2 * shift >= count
        if last:
            got_sum = lax.ppermute(fwd_sum, "seq", right)
            got_cot = lax.ppermute(bwd_sum, "seq", left)
        else:
            got_map, got_sum = lax.ppermute((fwd_map, fwd_sum), "seq", right)
            got_bmap, got_cot = lax.ppermute((bwd_map, bwd_sum), "seq", left)
        fwd_sum = mm("hij,hjk->hik", fwd_map, got_sum) + fwd_sum
        bwd_sum = mm("hji,hjk->hik", bwd_map, got_cot) + bwd_sum
        if not last:
            fwd_map = mm("hij,hjk->hik", fwd_map, got_map)
            bwd_map = mm("hij,hjk->hik", got_bmap, bwd_map)
        shift *= 2
    state_in = lax.ppermute(fwd_sum, "seq", [(i, i + 1) for i in range(count - 1)])
    end_cot = lax.ppermute(bwd_sum, "seq", [(i + 1, i) for i in range(count - 1)])
    return state_in, end_cot


def local(queries, reflect_keys, write_values, out_cotangent):
    tok_count, heads_here, head_size = queries.shape
    rows = 2 * tok_count
    q_raw = queries.astype(jnp.float32).transpose(1, 0, 2)
    cot = out_cotangent.astype(jnp.float32).transpose(1, 0, 2)
    k_raw = reflect_keys.astype(jnp.float32).reshape(rows, heads_here, head_size).transpose(1, 0, 2)
    vals = write_values.astype(jnp.float32).reshape(rows, heads_here, head_size).transpose(1, 0, 2)
    qn, q_scale = unit_rows(q_raw)
    kn, k_scale = unit_rows(k_raw)

    inverse = tri_inverse(kn)
    proj = mh("hij,hjd->hid", inverse, kn)
    upd_v = mh("hij,hjd->hid", inverse, vals)
    tok_ids = lax.broadcasted_iota(jnp.int32, (tok_count, rows), 0)
    sub_ids = lax.broadcasted_iota(jnp.int32, (tok_count, rows), 1)
    visible = sub_ids <= 2 * tok_ids + 1
    scores = jnp.where(visible, 2.0 * mh("hid,hjd->hij", qn, kn), 0.0)
    read_map = qn - mh("hij,hjd->hid", scores, proj)
    own_out = mh("hij,hjd->hid", scores, upd_v)
    eye = jnp.eye(head_size, dtype=jnp.float32)
    transition = eye - 2.0 * mh("hjd,hjw->hdw", kn, proj)
    offset = 2.0 * mh("hjd,hjw->hdw", kn, upd_v)
    local_cot = mh("hld,hlw->hdw", read_map, cot)

    state_in, end_cot = scan_seq(transition, offset, local_cot)

    produced = mh("hld,hdw->hlw", read_map, state_in) + own_out
    updates = upd_v - mh("hjd,hdw->hjw", proj, state_in)
    d_upd = mh("hij,hiw->hjw", scores, cot) + 2.0 * mh("hjd,hdw->hjw", kn, end_cot)
    d_w = mh("hij,hiw->hjw", inverse, d_upd)
    touch = jnp.where(visible, mh("hiw,hjw->hij", cot, updates), 0.0)
    d_qn = mh("hiw,hdw->hid", cot, state_in) + 2.0 * mh("hij,hjd->hid", touch, kn)
    gram_cot = jnp.where(strict_lower(rows, rows), -2.0 * mh("hiw,hjw->hij", d_w, updates), 0.0)
    d_kn = (
        2.0 * mh("hij,hid->hjd", touch, qn)
        + 2.0 * mh("hjw,hdw->hjd", updates, end_cot)
        - mh("hjw,hdw->hjd", d_w, state_in)
        + mh("hij,hjd->hid", gram_cot, kn)
        + mh("hji,hjd->hid", gram_cot, kn)
    )
    d_q = q_scale * (d_qn - jnp.sum(qn * d_qn, axis=-1, keepdims=True) * qn)
    d_k = k_scale * (d_kn - jnp.sum(kn * d_kn, axis=-1, keepdims=True) * kn)

    def token_major(tensor):
        return tensor.transpose(1, 0, 2).astype(jnp.bfloat16)

    def pair_major(tensor):
        return (
            tensor.reshape(heads_here, tok_count, 2, head_size)
            .transpose(1, 2, 0, 3)
            .astype(jnp.bfloat16)
        )

    return (token_major(produced), token_major(d_q), pair_major(d_k), pair_major(d_w))


def solution(mesh):
    in_specs = (
        P(("groups", "seq"), "head", None),
        P(("groups", "seq"), None, "head", None),
        P(("groups", "seq"), None, "head", None),
        P(("groups", "seq"), "head", None),
    )
    out_specs = (
        P(("groups", "seq"), "head", None),
        P(("groups", "seq"), "head", None),
        P(("groups", "seq"), None, "head", None),
        P(("groups", "seq"), None, "head", None),
    )
    return jax.shard_map(local, mesh=mesh, in_specs=in_specs, out_specs=out_specs, check_vma=False)
```

```python
import jax
import jax.numpy as jnp
from jax import lax
from jax.sharding import PartitionSpec as P

highest = lax.Precision.HIGHEST
LEAF = 16


def mm(spec, *operands):
    return jnp.einsum(spec, *operands, precision=highest)


def mh(spec, *operands):
    return jnp.einsum(spec, *operands, precision=lax.Precision.HIGH)


def unit_rows(tensor):
    scale = lax.rsqrt(jnp.sum(tensor * tensor, axis=-1, keepdims=True) + 1e-06)
    return tensor * scale, scale


def strict_lower(rows, cols):
    return lax.broadcasted_iota(jnp.int32, (rows, cols), 0) > lax.broadcasted_iota(
        jnp.int32, (rows, cols), 1
    )


def tri_inverse(keys):
    heads, rows, size = keys.shape
    tile = min(rows, 128)
    tiles = rows // tile
    tile_keys = keys.reshape(heads, tiles, tile, size)
    row = lax.broadcasted_iota(jnp.int32, (tile, tile), 0)
    col = lax.broadcasted_iota(jnp.int32, (tile, tile), 1)
    link = jnp.where(row > col, 2.0 * mm("htid,htjd->htij", tile_keys, tile_keys), 0.0)
    eye = jnp.eye(tile, dtype=jnp.float32)
    power = jnp.where(row // LEAF == col // LEAF, -link, 0.0)
    inverse = eye + power
    reach = 2
    while reach < LEAF:
        power = mm("htij,htjk->htik", power, power)
        inverse = inverse + mm("htij,htjk->htik", inverse, power)
        reach *= 2
    span = LEAF
    while span < tile:
        cross = (row // (2 * span) == col // (2 * span)) & (row // span != col // span)
        inverse = inverse - mm(
            "htij,htjk->htik", inverse, mm("htij,htjk->htik", jnp.where(cross, link, 0.0), inverse)
        )
        span *= 2
    if tiles == 1:
        return inverse.reshape(heads, rows, rows)
    blocks = {}
    for i in range(tiles):
        blocks[i, i] = inverse[:, i]
        for j in range(i - 1, -1, -1):
            acc = None
            for m in range(j, i):
                cross_link = 2.0 * mm("hid,hjd->hij", tile_keys[:, i], tile_keys[:, m])
                term = mm("hij,hjk->hik", cross_link, blocks[m, j])
                acc = term if acc is None else acc + term
            blocks[i, j] = -mm("hij,hjk->hik", blocks[i, i], acc)
    zero = jnp.zeros((heads, tile, tile), jnp.float32)
    band = [jnp.concatenate([blocks.get((i, j), zero) for j in range(tiles)], axis=2) for i in range(tiles)]
    return jnp.concatenate(band, axis=1)


def chain_seq(transition, offset, local_cot):
    count = lax.axis_size("seq")
    right = [(i, i + 1) for i in range(count - 1)]
    left = [(i + 1, i) for i in range(count - 1)]
    fwd_sum, bwd_sum = offset, local_cot
    for hop in range(count - 1):
        got_sum = lax.ppermute(fwd_sum, "seq", right)
        got_cot = lax.ppermute(bwd_sum, "seq", left)
        if hop == count - 2:
            return got_sum, got_cot
        fwd_sum = mm("hij,hjk->hik", transition, got_sum) + offset
        bwd_sum = mm("hji,hjk->hik", transition, got_cot) + local_cot
    zero = jnp.zeros_like(offset)
    return zero, zero


def scan_seq(transition, offset, local_cot):
    count = lax.axis_size("seq")
    if count <= 4:
        return chain_seq(transition, offset, local_cot)
    fwd_map, fwd_sum = transition, offset
    bwd_map, bwd_sum = transition, local_cot
    shift = 1
    while shift < count:
        right = [(i, i + shift) for i in range(count - shift)]
        left = [(i + shift, i) for i in range(count - shift)]
        last = 2 * shift >= count
        if last:
            got_sum = lax.ppermute(fwd_sum, "seq", right)
            got_cot = lax.ppermute(bwd_sum, "seq", left)
        else:
            got_map, got_sum = lax.ppermute((fwd_map, fwd_sum), "seq", right)
            got_bmap, got_cot = lax.ppermute((bwd_map, bwd_sum), "seq", left)
        fwd_sum = mm("hij,hjk->hik", fwd_map, got_sum) + fwd_sum
        bwd_sum = mm("hji,hjk->hik", bwd_map, got_cot) + bwd_sum
        if not last:
            fwd_map = mm("hij,hjk->hik", fwd_map, got_map)
            bwd_map = mm("hij,hjk->hik", got_bmap, bwd_map)
        shift *= 2
    state_in = lax.ppermute(fwd_sum, "seq", [(i, i + 1) for i in range(count - 1)])
    end_cot = lax.ppermute(bwd_sum, "seq", [(i + 1, i) for i in range(count - 1)])
    return state_in, end_cot


def local(queries, reflect_keys, write_values, out_cotangent):
    tok_count, heads_here, head_size = queries.shape
    rows = 2 * tok_count
    q_raw = queries.astype(jnp.float32).transpose(1, 0, 2)
    cot = out_cotangent.astype(jnp.float32).transpose(1, 0, 2)
    k_raw = reflect_keys.astype(jnp.float32).reshape(rows, heads_here, head_size).transpose(1, 0, 2)
    vals = write_values.astype(jnp.float32).reshape(rows, heads_here, head_size).transpose(1, 0, 2)
    qn, q_scale = unit_rows(q_raw)
    kn, k_scale = unit_rows(k_raw)

    inverse = tri_inverse(kn)
    proj = mh("hij,hjd->hid", inverse, kn)
    upd_v = mh("hij,hjd->hid", inverse, vals)
    tok_ids = lax.broadcasted_iota(jnp.int32, (tok_count, rows), 0)
    sub_ids = lax.broadcasted_iota(jnp.int32, (tok_count, rows), 1)
    visible = sub_ids <= 2 * tok_ids + 1
    scores = jnp.where(visible, 2.0 * mh("hid,hjd->hij", qn, kn), 0.0)
    read_map = qn - mh("hij,hjd->hid", scores, proj)
    own_out = mh("hij,hjd->hid", scores, upd_v)
    eye = jnp.eye(head_size, dtype=jnp.float32)
    transition = eye - 2.0 * mh("hjd,hjw->hdw", kn, proj)
    offset = 2.0 * mh("hjd,hjw->hdw", kn, upd_v)
    local_cot = mh("hld,hlw->hdw", read_map, cot)

    state_in, end_cot = scan_seq(transition, offset, local_cot)

    produced = mh("hld,hdw->hlw", read_map, state_in) + own_out
    updates = upd_v - mh("hjd,hdw->hjw", proj, state_in)
    d_upd = mh("hij,hiw->hjw", scores, cot) + 2.0 * mh("hjd,hdw->hjw", kn, end_cot)
    d_w = mh("hij,hiw->hjw", inverse, d_upd)
    touch = jnp.where(visible, mh("hiw,hjw->hij", cot, updates), 0.0)
    d_qn = mh("hiw,hdw->hid", cot, state_in) + 2.0 * mh("hij,hjd->hid", touch, kn)
    gram_cot = jnp.where(strict_lower(rows, rows), -2.0 * mh("hiw,hjw->hij", d_w, updates), 0.0)
    d_kn = (
        2.0 * mh("hij,hid->hjd", touch, qn)
        + 2.0 * mh("hjw,hdw->hjd", updates, end_cot)
        - mh("hjw,hdw->hjd", d_w, state_in)
        + mh("hij,hjd->hid", gram_cot, kn)
        + mh("hji,hjd->hid", gram_cot, kn)
    )
    d_q = q_scale * (d_qn - jnp.sum(qn * d_qn, axis=-1, keepdims=True) * qn)
    d_k = k_scale * (d_kn - jnp.sum(kn * d_kn, axis=-1, keepdims=True) * kn)

    def token_major(tensor):
        return tensor.transpose(1, 0, 2).astype(jnp.bfloat16)

    def pair_major(tensor):
        return (
            tensor.reshape(heads_here, tok_count, 2, head_size)
            .transpose(1, 2, 0, 3)
            .astype(jnp.bfloat16)
        )

    return (token_major(produced), token_major(d_q), pair_major(d_k), pair_major(d_w))


def solution(mesh):
    in_specs = (
        P(("groups", "seq"), "head", None),
        P(("groups", "seq"), None, "head", None),
        P(("groups", "seq"), None, "head", None),
        P(("groups", "seq"), "head", None),
    )
    out_specs = (
        P(("groups", "seq"), "head", None),
        P(("groups", "seq"), "head", None),
        P(("groups", "seq"), None, "head", None),
        P(("groups", "seq"), None, "head", None),
    )
    return jax.shard_map(local, mesh=mesh, in_specs=in_specs, out_specs=out_specs, check_vma=False)
```

```python
import jax
import jax.numpy as jnp
from jax import lax
from jax.sharding import PartitionSpec as P

highest = lax.Precision.HIGHEST
LEAF = 16


def mm(spec, *operands):
    return jnp.einsum(spec, *operands, precision=highest)


def mh(spec, *operands):
    return jnp.einsum(spec, *operands, precision=lax.Precision.HIGH)


def unit_rows(tensor):
    scale = lax.rsqrt(jnp.sum(tensor * tensor, axis=-1, keepdims=True) + 1e-06)
    return tensor * scale, scale


def strict_lower(rows, cols):
    return lax.broadcasted_iota(jnp.int32, (rows, cols), 0) > lax.broadcasted_iota(
        jnp.int32, (rows, cols), 1
    )


def tri_inverse(keys):
    heads, rows, size = keys.shape
    leaves = rows // LEAF
    leaf_keys = keys.reshape(heads, leaves, LEAF, size)
    gram = mm("hpid,hpjd->hpij", leaf_keys, leaf_keys)
    power = jnp.where(strict_lower(LEAF, LEAF), -2.0 * gram, 0.0)
    eye = jnp.eye(LEAF, dtype=jnp.float32)
    inverse = eye + power
    reach = 2
    while reach < LEAF:
        power = mm("hpij,hpjk->hpik", power, power)
        inverse = inverse + mm("hpij,hpjk->hpik", inverse, power)
        reach *= 2
    span = LEAF
    while span < rows:
        pairs = rows // (2 * span)
        blocks = inverse.reshape(heads, pairs, 2, span, span)
        upper_inv = blocks[:, :, 0]
        lower_inv = blocks[:, :, 1]
        halves = keys.reshape(heads, pairs, 2, span, size)
        link = 2.0 * mm("hpid,hpjd->hpij", halves[:, :, 1], halves[:, :, 0])
        corner = -mm("hpij,hpjk->hpik", lower_inv, mm("hpij,hpjk->hpik", link, upper_inv))
        top = jnp.concatenate([upper_inv, jnp.zeros_like(upper_inv)], axis=3)
        bottom = jnp.concatenate([corner, lower_inv], axis=3)
        inverse = jnp.concatenate([top, bottom], axis=2)
        span *= 2
    return inverse.reshape(heads, rows, rows)


def chain_seq(transition, offset, local_cot):
    count = lax.axis_size("seq")
    right = [(i, i + 1) for i in range(count - 1)]
    left = [(i + 1, i) for i in range(count - 1)]
    fwd_sum, bwd_sum = offset, local_cot
    for hop in range(count - 1):
        got_sum = lax.ppermute(fwd_sum, "seq", right)
        got_cot = lax.ppermute(bwd_sum, "seq", left)
        if hop == count - 2:
            return got_sum, got_cot
        fwd_sum = mm("hij,hjk->hik", transition, got_sum) + offset
        bwd_sum = mm("hji,hjk->hik", transition, got_cot) + local_cot
    zero = jnp.zeros_like(offset)
    return zero, zero


def scan_seq(transition, offset, local_cot):
    count = lax.axis_size("seq")
    if count <= 4:
        return chain_seq(transition, offset, local_cot)
    fwd_map, fwd_sum = transition, offset
    bwd_map, bwd_sum = transition, local_cot
    shift = 1
    while shift < count:
        right = [(i, i + shift) for i in range(count - shift)]
        left = [(i + shift, i) for i in range(count - shift)]
        last = 2 * shift >= count
        if last:
            got_sum = lax.ppermute(fwd_sum, "seq", right)
            got_cot = lax.ppermute(bwd_sum, "seq", left)
        else:
            got_map, got_sum = lax.ppermute((fwd_map, fwd_sum), "seq", right)
            got_bmap, got_cot = lax.ppermute((bwd_map, bwd_sum), "seq", left)
        fwd_sum = mm("hij,hjk->hik", fwd_map, got_sum) + fwd_sum
        bwd_sum = mm("hji,hjk->hik", bwd_map, got_cot) + bwd_sum
        if not last:
            fwd_map = mm("hij,hjk->hik", fwd_map, got_map)
            bwd_map = mm("hij,hjk->hik", got_bmap, bwd_map)
        shift *= 2
    state_in = lax.ppermute(fwd_sum, "seq", [(i, i + 1) for i in range(count - 1)])
    end_cot = lax.ppermute(bwd_sum, "seq", [(i + 1, i) for i in range(count - 1)])
    return state_in, end_cot


def local(queries, reflect_keys, write_values, out_cotangent):
    tok_count, heads_here, head_size = queries.shape
    rows = 2 * tok_count
    q_raw = queries.astype(jnp.float32).transpose(1, 0, 2)
    cot = out_cotangent.astype(jnp.float32).transpose(1, 0, 2)
    k_raw = reflect_keys.astype(jnp.float32).reshape(rows, heads_here, head_size).transpose(1, 0, 2)
    vals = write_values.astype(jnp.float32).reshape(rows, heads_here, head_size).transpose(1, 0, 2)
    qn, q_scale = unit_rows(q_raw)
    kn, k_scale = unit_rows(k_raw)

    inverse = tri_inverse(kn)
    solved = mh("hij,hjd->hid", inverse, jnp.concatenate([kn, vals], axis=2))
    proj = solved[:, :, :head_size]
    upd_v = solved[:, :, head_size:]
    tok_ids = lax.broadcasted_iota(jnp.int32, (tok_count, rows), 0)
    sub_ids = lax.broadcasted_iota(jnp.int32, (tok_count, rows), 1)
    visible = sub_ids <= 2 * tok_ids + 1
    scores = jnp.where(visible, 2.0 * mh("hid,hjd->hij", qn, kn), 0.0)
    seen = mh("hij,hjd->hid", scores, solved)
    read_map = qn - seen[:, :, :head_size]
    own_out = seen[:, :, head_size:]
    eye = jnp.eye(head_size, dtype=jnp.float32)
    moved = 2.0 * mh("hjd,hjw->hdw", kn, solved)
    transition = eye - moved[:, :, :head_size]
    offset = moved[:, :, head_size:]
    local_cot = mh("hld,hlw->hdw", read_map, cot)

    state_in, end_cot = scan_seq(transition, offset, local_cot)

    produced = mh("hld,hdw->hlw", read_map, state_in) + own_out
    updates = upd_v - mh("hjd,hdw->hjw", proj, state_in)
    d_upd = mh("hij,hiw->hjw", scores, cot) + 2.0 * mh("hjd,hdw->hjw", kn, end_cot)
    d_w = mh("hij,hiw->hjw", inverse, d_upd)
    touch = jnp.where(visible, mh("hiw,hjw->hij", cot, updates), 0.0)
    d_qn = mh("hiw,hdw->hid", cot, state_in) + 2.0 * mh("hij,hjd->hid", touch, kn)
    gram_cot = jnp.where(strict_lower(rows, rows), -2.0 * mh("hiw,hjw->hij", d_w, updates), 0.0)
    d_kn = (
        2.0 * mh("hij,hid->hjd", touch, qn)
        + 2.0 * mh("hjw,hdw->hjd", updates, end_cot)
        - mh("hjw,hdw->hjd", d_w, state_in)
        + mh("hij,hjd->hid", gram_cot + gram_cot.transpose(0, 2, 1), kn)
    )
    d_q = q_scale * (d_qn - jnp.sum(qn * d_qn, axis=-1, keepdims=True) * qn)
    d_k = k_scale * (d_kn - jnp.sum(kn * d_kn, axis=-1, keepdims=True) * kn)

    def token_major(tensor):
        return tensor.transpose(1, 0, 2).astype(jnp.bfloat16)

    def pair_major(tensor):
        return (
            tensor.reshape(heads_here, tok_count, 2, head_size)
            .transpose(1, 2, 0, 3)
            .astype(jnp.bfloat16)
        )

    return (token_major(produced), token_major(d_q), pair_major(d_k), pair_major(d_w))


def solution(mesh):
    in_specs = (
        P(("groups", "seq"), "head", None),
        P(("groups", "seq"), None, "head", None),
        P(("groups", "seq"), None, "head", None),
        P(("groups", "seq"), "head", None),
    )
    out_specs = (
        P(("groups", "seq"), "head", None),
        P(("groups", "seq"), "head", None),
        P(("groups", "seq"), None, "head", None),
        P(("groups", "seq"), None, "head", None),
    )
    return jax.shard_map(local, mesh=mesh, in_specs=in_specs, out_specs=out_specs, check_vma=False)
```

```python
import jax
import jax.numpy as jnp
from jax import lax
from jax.experimental import pallas as pl
from jax.sharding import PartitionSpec as P

highest = lax.Precision.HIGHEST
LEAF = 16


def mm(spec, *operands):
    return jnp.einsum(spec, *operands, precision=highest)


def mh(spec, *operands):
    return jnp.einsum(spec, *operands, precision=lax.Precision.HIGH)


def unit_rows(tensor):
    scale = lax.rsqrt(jnp.sum(tensor * tensor, axis=-1, keepdims=True) + 1e-06)
    return tensor * scale, scale


def strict_lower(rows, cols):
    return lax.broadcasted_iota(jnp.int32, (rows, cols), 0) > lax.broadcasted_iota(
        jnp.int32, (rows, cols), 1
    )


TILE = 128


def dot(left, right, t_right=False):
    dims = (((1,), (1 if t_right else 0,)), ((), ()))
    return lax.dot_general(left, right, dims, precision=highest, preferred_element_type=jnp.float32)


def inverse_kernel(k_ref, inv_ref):
    heads, rows, size = k_ref.shape
    tiles = rows // TILE
    row = lax.broadcasted_iota(jnp.int32, (TILE, TILE), 0)
    col = lax.broadcasted_iota(jnp.int32, (TILE, TILE), 1)
    eye = jnp.where(row == col, 1.0, 0.0).astype(jnp.float32)
    chains = [(h, t) for h in range(heads) for t in range(tiles)]
    keys = {(h, t): k_ref[h, t * TILE:(t + 1) * TILE, :] for h, t in chains}
    link = {c: jnp.where(row > col, 2.0 * dot(keys[c], keys[c], t_right=True), 0.0) for c in chains}
    power = {c: jnp.where(row // LEAF == col // LEAF, -link[c], 0.0) for c in chains}
    inverse = {c: eye + power[c] for c in chains}
    reach = 2
    while reach < LEAF:
        power = {c: dot(power[c], power[c]) for c in chains}
        inverse = {c: inverse[c] + dot(inverse[c], power[c]) for c in chains}
        reach *= 2
    span = LEAF
    while span < TILE:
        cross = (row // (2 * span) == col // (2 * span)) & (row // span != col // span)
        inner = {c: dot(jnp.where(cross, link[c], 0.0), inverse[c]) for c in chains}
        inverse = {c: inverse[c] - dot(inverse[c], inner[c]) for c in chains}
        span *= 2
    blocks = {}
    for h in range(heads):
        for t in range(tiles):
            blocks[h, t, t] = inverse[h, t]
    for i in range(tiles):
        for j in range(i - 1, -1, -1):
            for h in range(heads):
                acc = None
                for m in range(j, i):
                    term = dot(2.0 * dot(keys[h, i], keys[h, m], t_right=True), blocks[h, m, j])
                    acc = term if acc is None else acc + term
                blocks[h, i, j] = -dot(blocks[h, i, i], acc)
    zero = jnp.zeros((TILE, TILE), jnp.float32)
    for h in range(heads):
        for i in range(tiles):
            for j in range(tiles):
                inv_ref[h, i * TILE:(i + 1) * TILE, j * TILE:(j + 1) * TILE] = blocks.get((h, i, j), zero)


def tri_inverse(keys):
    heads, rows, size = keys.shape
    return pl.pallas_call(
        inverse_kernel,
        out_shape=jax.ShapeDtypeStruct((heads, rows, rows), jnp.float32),
    )(keys)


def chain_seq(transition, offset, local_cot):
    count = lax.axis_size("seq")
    right = [(i, i + 1) for i in range(count - 1)]
    left = [(i + 1, i) for i in range(count - 1)]
    fwd_sum, bwd_sum = offset, local_cot
    for hop in range(count - 1):
        got_sum = lax.ppermute(fwd_sum, "seq", right)
        got_cot = lax.ppermute(bwd_sum, "seq", left)
        if hop == count - 2:
            return got_sum, got_cot
        fwd_sum = mm("hij,hjk->hik", transition, got_sum) + offset
        bwd_sum = mm("hji,hjk->hik", transition, got_cot) + local_cot
    zero = jnp.zeros_like(offset)
    return zero, zero


def scan_seq(transition, offset, local_cot):
    count = lax.axis_size("seq")
    if count <= 4:
        return chain_seq(transition, offset, local_cot)
    fwd_map, fwd_sum = transition, offset
    bwd_map, bwd_sum = transition, local_cot
    shift = 1
    while shift < count:
        right = [(i, i + shift) for i in range(count - shift)]
        left = [(i + shift, i) for i in range(count - shift)]
        last = 2 * shift >= count
        if last:
            got_sum = lax.ppermute(fwd_sum, "seq", right)
            got_cot = lax.ppermute(bwd_sum, "seq", left)
        else:
            got_map, got_sum = lax.ppermute((fwd_map, fwd_sum), "seq", right)
            got_bmap, got_cot = lax.ppermute((bwd_map, bwd_sum), "seq", left)
        fwd_sum = mm("hij,hjk->hik", fwd_map, got_sum) + fwd_sum
        bwd_sum = mm("hji,hjk->hik", bwd_map, got_cot) + bwd_sum
        if not last:
            fwd_map = mm("hij,hjk->hik", fwd_map, got_map)
            bwd_map = mm("hij,hjk->hik", got_bmap, bwd_map)
        shift *= 2
    state_in = lax.ppermute(fwd_sum, "seq", [(i, i + 1) for i in range(count - 1)])
    end_cot = lax.ppermute(bwd_sum, "seq", [(i + 1, i) for i in range(count - 1)])
    return state_in, end_cot


def local(queries, reflect_keys, write_values, out_cotangent):
    tok_count, heads_here, head_size = queries.shape
    rows = 2 * tok_count
    q_raw = queries.astype(jnp.float32).transpose(1, 0, 2)
    cot = out_cotangent.astype(jnp.float32).transpose(1, 0, 2)
    k_raw = reflect_keys.astype(jnp.float32).reshape(rows, heads_here, head_size).transpose(1, 0, 2)
    vals = write_values.astype(jnp.float32).reshape(rows, heads_here, head_size).transpose(1, 0, 2)
    qn, q_scale = unit_rows(q_raw)
    kn, k_scale = unit_rows(k_raw)

    inverse = tri_inverse(kn)
    proj = mh("hij,hjd->hid", inverse, kn)
    upd_v = mh("hij,hjd->hid", inverse, vals)
    tok_ids = lax.broadcasted_iota(jnp.int32, (tok_count, rows), 0)
    sub_ids = lax.broadcasted_iota(jnp.int32, (tok_count, rows), 1)
    visible = sub_ids <= 2 * tok_ids + 1
    scores = jnp.where(visible, 2.0 * mh("hid,hjd->hij", qn, kn), 0.0)
    read_map = qn - mh("hij,hjd->hid", scores, proj)
    own_out = mh("hij,hjd->hid", scores, upd_v)
    eye = jnp.eye(head_size, dtype=jnp.float32)
    transition = eye - 2.0 * mh("hjd,hjw->hdw", kn, proj)
    offset = 2.0 * mh("hjd,hjw->hdw", kn, upd_v)
    local_cot = mh("hld,hlw->hdw", read_map, cot)

    state_in, end_cot = scan_seq(transition, offset, local_cot)

    produced = mh("hld,hdw->hlw", read_map, state_in) + own_out
    updates = upd_v - mh("hjd,hdw->hjw", proj, state_in)
    d_upd = mh("hij,hiw->hjw", scores, cot) + 2.0 * mh("hjd,hdw->hjw", kn, end_cot)
    d_w = mh("hij,hiw->hjw", inverse, d_upd)
    touch = jnp.where(visible, mh("hiw,hjw->hij", cot, updates), 0.0)
    d_qn = mh("hiw,hdw->hid", cot, state_in) + 2.0 * mh("hij,hjd->hid", touch, kn)
    gram_cot = jnp.where(strict_lower(rows, rows), -2.0 * mh("hiw,hjw->hij", d_w, updates), 0.0)
    d_kn = (
        2.0 * mh("hij,hid->hjd", touch, qn)
        + 2.0 * mh("hjw,hdw->hjd", updates, end_cot)
        - mh("hjw,hdw->hjd", d_w, state_in)
        + mh("hij,hjd->hid", gram_cot, kn)
        + mh("hji,hjd->hid", gram_cot, kn)
    )
    d_q = q_scale * (d_qn - jnp.sum(qn * d_qn, axis=-1, keepdims=True) * qn)
    d_k = k_scale * (d_kn - jnp.sum(kn * d_kn, axis=-1, keepdims=True) * kn)

    def token_major(tensor):
        return tensor.transpose(1, 0, 2).astype(jnp.bfloat16)

    def pair_major(tensor):
        return (
            tensor.reshape(heads_here, tok_count, 2, head_size)
            .transpose(1, 2, 0, 3)
            .astype(jnp.bfloat16)
        )

    return (token_major(produced), token_major(d_q), pair_major(d_k), pair_major(d_w))


def solution(mesh):
    in_specs = (
        P(("groups", "seq"), "head", None),
        P(("groups", "seq"), None, "head", None),
        P(("groups", "seq"), None, "head", None),
        P(("groups", "seq"), "head", None),
    )
    out_specs = (
        P(("groups", "seq"), "head", None),
        P(("groups", "seq"), "head", None),
        P(("groups", "seq"), None, "head", None),
        P(("groups", "seq"), None, "head", None),
    )
    return jax.shard_map(local, mesh=mesh, in_specs=in_specs, out_specs=out_specs, check_vma=False)
```

```python
import jax
import jax.numpy as jnp
from jax import lax
from jax.sharding import PartitionSpec as P

highest = lax.Precision.HIGHEST
LEAF = 16


def mm(spec, *operands):
    return jnp.einsum(spec, *operands, precision=highest)


def mh(spec, *operands):
    return jnp.einsum(spec, *operands, precision=lax.Precision.HIGH)


def unit_rows(tensor):
    scale = lax.rsqrt(jnp.sum(tensor * tensor, axis=-1, keepdims=True) + 1e-06)
    return tensor * scale, scale


def strict_lower(rows, cols):
    return lax.broadcasted_iota(jnp.int32, (rows, cols), 0) > lax.broadcasted_iota(
        jnp.int32, (rows, cols), 1
    )


def tri_inverse(keys):
    heads, rows, size = keys.shape
    leaves = rows // LEAF
    leaf_keys = keys.reshape(heads, leaves, LEAF, size)
    gram = mm("hpid,hpjd->hpij", leaf_keys, leaf_keys)
    power = jnp.where(strict_lower(LEAF, LEAF), -2.0 * gram, 0.0)
    eye = jnp.eye(LEAF, dtype=jnp.float32)
    inverse = eye + power
    reach = 2
    while reach < LEAF:
        power = mm("hpij,hpjk->hpik", power, power)
        inverse = inverse + mm("hpij,hpjk->hpik", inverse, power)
        reach *= 2
    span = LEAF
    while span < rows:
        pairs = rows // (2 * span)
        blocks = inverse.reshape(heads, pairs, 2, span, span)
        upper_inv = blocks[:, :, 0]
        lower_inv = blocks[:, :, 1]
        halves = keys.reshape(heads, pairs, 2, span, size)
        link = 2.0 * mm("hpid,hpjd->hpij", halves[:, :, 1], halves[:, :, 0])
        corner = -mm("hpij,hpjk->hpik", lower_inv, mm("hpij,hpjk->hpik", link, upper_inv))
        top = jnp.concatenate([upper_inv, jnp.zeros_like(upper_inv)], axis=3)
        bottom = jnp.concatenate([corner, lower_inv], axis=3)
        inverse = jnp.concatenate([top, bottom], axis=2)
        span *= 2
    return inverse.reshape(heads, rows, rows)


def chain_seq(transition, offset, local_cot):
    count = lax.axis_size("seq")
    right = [(i, i + 1) for i in range(count - 1)]
    left = [(i + 1, i) for i in range(count - 1)]
    offset, local_cot = lax.optimization_barrier((offset, local_cot))
    fwd_sum, bwd_sum = offset, local_cot
    for hop in range(count - 1):
        got_sum = lax.ppermute(fwd_sum, "seq", right)
        got_cot = lax.ppermute(bwd_sum, "seq", left)
        if hop == count - 2:
            return got_sum, got_cot
        fwd_sum = mm("hij,hjk->hik", transition, got_sum) + offset
        bwd_sum = mm("hji,hjk->hik", transition, got_cot) + local_cot
    zero = jnp.zeros_like(offset)
    return zero, zero


def scan_seq(transition, offset, local_cot):
    count = lax.axis_size("seq")
    if count <= 4:
        return chain_seq(transition, offset, local_cot)
    fwd_map, fwd_sum = transition, offset
    bwd_map, bwd_sum = transition, local_cot
    shift = 1
    while shift < count:
        right = [(i, i + shift) for i in range(count - shift)]
        left = [(i + shift, i) for i in range(count - shift)]
        last = 2 * shift >= count
        if last:
            got_sum = lax.ppermute(fwd_sum, "seq", right)
            got_cot = lax.ppermute(bwd_sum, "seq", left)
        else:
            got_map, got_sum = lax.ppermute((fwd_map, fwd_sum), "seq", right)
            got_bmap, got_cot = lax.ppermute((bwd_map, bwd_sum), "seq", left)
        fwd_sum = mm("hij,hjk->hik", fwd_map, got_sum) + fwd_sum
        bwd_sum = mm("hji,hjk->hik", bwd_map, got_cot) + bwd_sum
        if not last:
            fwd_map = mm("hij,hjk->hik", fwd_map, got_map)
            bwd_map = mm("hij,hjk->hik", got_bmap, bwd_map)
        shift *= 2
    state_in = lax.ppermute(fwd_sum, "seq", [(i, i + 1) for i in range(count - 1)])
    end_cot = lax.ppermute(bwd_sum, "seq", [(i + 1, i) for i in range(count - 1)])
    return state_in, end_cot


def local(queries, reflect_keys, write_values, out_cotangent):
    tok_count, heads_here, head_size = queries.shape
    rows = 2 * tok_count
    q_raw = queries.astype(jnp.float32).transpose(1, 0, 2)
    cot = out_cotangent.astype(jnp.float32).transpose(1, 0, 2)
    k_raw = reflect_keys.astype(jnp.float32).reshape(rows, heads_here, head_size).transpose(1, 0, 2)
    vals = write_values.astype(jnp.float32).reshape(rows, heads_here, head_size).transpose(1, 0, 2)
    qn, q_scale = unit_rows(q_raw)
    kn, k_scale = unit_rows(k_raw)

    inverse = tri_inverse(kn)
    proj = mh("hij,hjd->hid", inverse, kn)
    upd_v = mh("hij,hjd->hid", inverse, vals)
    tok_ids = lax.broadcasted_iota(jnp.int32, (tok_count, rows), 0)
    sub_ids = lax.broadcasted_iota(jnp.int32, (tok_count, rows), 1)
    visible = sub_ids <= 2 * tok_ids + 1
    scores = jnp.where(visible, 2.0 * mh("hid,hjd->hij", qn, kn), 0.0)
    read_map = qn - mh("hij,hjd->hid", scores, proj)
    own_out = mh("hij,hjd->hid", scores, upd_v)
    eye = jnp.eye(head_size, dtype=jnp.float32)
    transition = eye - 2.0 * mh("hjd,hjw->hdw", kn, proj)
    offset = 2.0 * mh("hjd,hjw->hdw", kn, upd_v)
    local_cot = mh("hld,hlw->hdw", read_map, cot)

    state_in, end_cot = scan_seq(transition, offset, local_cot)

    produced = mh("hld,hdw->hlw", read_map, state_in) + own_out
    updates = upd_v - mh("hjd,hdw->hjw", proj, state_in)
    d_upd = mh("hij,hiw->hjw", scores, cot) + 2.0 * mh("hjd,hdw->hjw", kn, end_cot)
    d_w = mh("hij,hiw->hjw", inverse, d_upd)
    touch = jnp.where(visible, mh("hiw,hjw->hij", cot, updates), 0.0)
    d_qn = mh("hiw,hdw->hid", cot, state_in) + 2.0 * mh("hij,hjd->hid", touch, kn)
    gram_cot = jnp.where(strict_lower(rows, rows), -2.0 * mh("hiw,hjw->hij", d_w, updates), 0.0)
    d_kn = (
        2.0 * mh("hij,hid->hjd", touch, qn)
        + 2.0 * mh("hjw,hdw->hjd", updates, end_cot)
        - mh("hjw,hdw->hjd", d_w, state_in)
        + mh("hij,hjd->hid", gram_cot, kn)
        + mh("hji,hjd->hid", gram_cot, kn)
    )
    d_q = q_scale * (d_qn - jnp.sum(qn * d_qn, axis=-1, keepdims=True) * qn)
    d_k = k_scale * (d_kn - jnp.sum(kn * d_kn, axis=-1, keepdims=True) * kn)

    def token_major(tensor):
        return tensor.transpose(1, 0, 2).astype(jnp.bfloat16)

    def pair_major(tensor):
        return (
            tensor.reshape(heads_here, tok_count, 2, head_size)
            .transpose(1, 2, 0, 3)
            .astype(jnp.bfloat16)
        )

    return (token_major(produced), token_major(d_q), pair_major(d_k), pair_major(d_w))


def solution(mesh):
    in_specs = (
        P(("groups", "seq"), "head", None),
        P(("groups", "seq"), None, "head", None),
        P(("groups", "seq"), None, "head", None),
        P(("groups", "seq"), "head", None),
    )
    out_specs = (
        P(("groups", "seq"), "head", None),
        P(("groups", "seq"), "head", None),
        P(("groups", "seq"), None, "head", None),
        P(("groups", "seq"), None, "head", None),
    )
    return jax.shard_map(local, mesh=mesh, in_specs=in_specs, out_specs=out_specs, check_vma=False)
```

```python
import jax
import jax.numpy as jnp
from jax import lax
from jax.sharding import PartitionSpec as P

highest = lax.Precision.HIGHEST
LEAF = 16


def mm(spec, *operands):
    return jnp.einsum(spec, *operands, precision=highest)


def mh(spec, *operands):
    return jnp.einsum(spec, *operands, precision=lax.Precision.HIGH)


def unit_rows(tensor):
    scale = lax.rsqrt(jnp.sum(tensor * tensor, axis=-1, keepdims=True) + 1e-06)
    return tensor * scale, scale


def strict_lower(rows, cols):
    return lax.broadcasted_iota(jnp.int32, (rows, cols), 0) > lax.broadcasted_iota(
        jnp.int32, (rows, cols), 1
    )


def tri_inverse(keys):
    heads, rows, size = keys.shape
    leaves = rows // LEAF
    leaf_keys = keys.reshape(heads, leaves, LEAF, size)
    gram = mm("hpid,hpjd->hpij", leaf_keys, leaf_keys)
    power = jnp.where(strict_lower(LEAF, LEAF), -2.0 * gram, 0.0)
    eye = jnp.eye(LEAF, dtype=jnp.float32)
    inverse = eye + power
    reach = 2
    while reach < LEAF:
        power = mm("hpij,hpjk->hpik", power, power)
        inverse = inverse + mm("hpij,hpjk->hpik", inverse, power)
        reach *= 2
    span = LEAF
    while span < rows:
        pairs = rows // (2 * span)
        blocks = inverse.reshape(heads, pairs, 2, span, span)
        upper_inv = blocks[:, :, 0]
        lower_inv = blocks[:, :, 1]
        halves = keys.reshape(heads, pairs, 2, span, size)
        link = 2.0 * mm("hpid,hpjd->hpij", halves[:, :, 1], halves[:, :, 0])
        corner = -mm("hpij,hpjk->hpik", lower_inv, mm("hpij,hpjk->hpik", link, upper_inv))
        top = jnp.concatenate([upper_inv, jnp.zeros_like(upper_inv)], axis=3)
        bottom = jnp.concatenate([corner, lower_inv], axis=3)
        inverse = jnp.concatenate([top, bottom], axis=2)
        span *= 2
    return inverse.reshape(heads, rows, rows)


def chain_seq(transition, offset, local_cot):
    count = lax.axis_size("seq")
    right = [(i, i + 1) for i in range(count - 1)]
    left = [(i + 1, i) for i in range(count - 1)]
    fwd_sum, bwd_sum = offset, local_cot
    for hop in range(count - 1):
        got_sum = lax.ppermute(fwd_sum, "seq", right)
        got_cot = lax.ppermute(bwd_sum, "seq", left)
        if hop == count - 2:
            return got_sum, got_cot
        fwd_sum = mm("hij,hjk->hik", transition, got_sum) + offset
        bwd_sum = mm("hji,hjk->hik", transition, got_cot) + local_cot
    zero = jnp.zeros_like(offset)
    return zero, zero


def scan_seq(transition, offset, local_cot):
    count = lax.axis_size("seq")
    if count <= 4:
        return chain_seq(transition, offset, local_cot)
    fwd_map, fwd_sum = transition, offset
    bwd_map, bwd_sum = transition, local_cot
    shift = 1
    while shift < count:
        right = [(i, i + shift) for i in range(count - shift)]
        left = [(i + shift, i) for i in range(count - shift)]
        last = 2 * shift >= count
        if last:
            got_sum = lax.ppermute(fwd_sum, "seq", right)
            got_cot = lax.ppermute(bwd_sum, "seq", left)
        else:
            got_map, got_sum = lax.ppermute((fwd_map, fwd_sum), "seq", right)
            got_bmap, got_cot = lax.ppermute((bwd_map, bwd_sum), "seq", left)
        fwd_sum = mm("hij,hjk->hik", fwd_map, got_sum) + fwd_sum
        bwd_sum = mm("hji,hjk->hik", bwd_map, got_cot) + bwd_sum
        if not last:
            fwd_map = mm("hij,hjk->hik", fwd_map, got_map)
            bwd_map = mm("hij,hjk->hik", got_bmap, bwd_map)
        shift *= 2
    state_in = lax.ppermute(fwd_sum, "seq", [(i, i + 1) for i in range(count - 1)])
    end_cot = lax.ppermute(bwd_sum, "seq", [(i + 1, i) for i in range(count - 1)])
    return state_in, end_cot


def local(queries, reflect_keys, write_values, out_cotangent):
    tok_count, heads_here, head_size = queries.shape
    rows = 2 * tok_count
    q_raw = queries.astype(jnp.float32).transpose(1, 0, 2)
    cot = out_cotangent.astype(jnp.float32).transpose(1, 0, 2)
    k_raw = reflect_keys.astype(jnp.float32).reshape(rows, heads_here, head_size).transpose(1, 0, 2)
    vals = write_values.astype(jnp.float32).reshape(rows, heads_here, head_size).transpose(1, 0, 2)
    qn, q_scale = unit_rows(q_raw)
    kn, k_scale = unit_rows(k_raw)

    inverse = tri_inverse(kn)
    proj = mh("hij,hjd->hid", inverse, kn)
    upd_v = mh("hij,hjd->hid", inverse, vals)
    tok_ids = lax.broadcasted_iota(jnp.int32, (tok_count, rows), 0)
    sub_ids = lax.broadcasted_iota(jnp.int32, (tok_count, rows), 1)
    visible = sub_ids <= 2 * tok_ids + 1
    scores = jnp.where(visible, 2.0 * mh("hid,hjd->hij", qn, kn), 0.0)
    read_map = qn - mh("hij,hjd->hid", scores, proj)
    own_out = mh("hij,hjd->hid", scores, upd_v)
    eye = jnp.eye(head_size, dtype=jnp.float32)
    transition = eye - 2.0 * mh("hjd,hjw->hdw", kn, proj)
    offset = 2.0 * mh("hjd,hjw->hdw", kn, upd_v)
    local_cot = mh("hld,hlw->hdw", read_map, cot)

    state_in, end_cot = scan_seq(transition, offset, local_cot)

    produced = mh("hld,hdw->hlw", read_map, state_in) + own_out
    updates = upd_v - mh("hjd,hdw->hjw", proj, state_in)
    w_cot = mh("hij,hiw->hjw", inverse, mh("hij,hiw->hjw", scores, cot))
    w_key = 2.0 * mh("hij,hid->hjd", inverse, kn)
    d_w = w_cot + mh("hjd,hdw->hjw", w_key, end_cot)
    touch = jnp.where(visible, mh("hiw,hjw->hij", cot, updates), 0.0)
    d_qn = mh("hiw,hdw->hid", cot, state_in) + 2.0 * mh("hij,hjd->hid", touch, kn)
    gram_cot = jnp.where(strict_lower(rows, rows), -2.0 * mh("hiw,hjw->hij", d_w, updates), 0.0)
    d_kn = (
        2.0 * mh("hij,hid->hjd", touch, qn)
        + 2.0 * mh("hjw,hdw->hjd", updates, end_cot)
        - mh("hjw,hdw->hjd", d_w, state_in)
        + mh("hij,hjd->hid", gram_cot, kn)
        + mh("hji,hjd->hid", gram_cot, kn)
    )
    d_q = q_scale * (d_qn - jnp.sum(qn * d_qn, axis=-1, keepdims=True) * qn)
    d_k = k_scale * (d_kn - jnp.sum(kn * d_kn, axis=-1, keepdims=True) * kn)

    def token_major(tensor):
        return tensor.transpose(1, 0, 2).astype(jnp.bfloat16)

    def pair_major(tensor):
        return (
            tensor.reshape(heads_here, tok_count, 2, head_size)
            .transpose(1, 2, 0, 3)
            .astype(jnp.bfloat16)
        )

    return (token_major(produced), token_major(d_q), pair_major(d_k), pair_major(d_w))


def solution(mesh):
    in_specs = (
        P(("groups", "seq"), "head", None),
        P(("groups", "seq"), None, "head", None),
        P(("groups", "seq"), None, "head", None),
        P(("groups", "seq"), "head", None),
    )
    out_specs = (
        P(("groups", "seq"), "head", None),
        P(("groups", "seq"), "head", None),
        P(("groups", "seq"), None, "head", None),
        P(("groups", "seq"), None, "head", None),
    )
    return jax.shard_map(local, mesh=mesh, in_specs=in_specs, out_specs=out_specs, check_vma=False)
```

```python
import jax
import jax.numpy as jnp
from jax import lax
from jax.sharding import PartitionSpec as P

highest = lax.Precision.HIGHEST
LEAF = 16


def mm(spec, *operands):
    return jnp.einsum(spec, *operands, precision=highest)


def mh(spec, *operands):
    return jnp.einsum(spec, *operands, precision=lax.Precision.HIGH)


def unit_rows(tensor):
    scale = lax.rsqrt(jnp.sum(tensor * tensor, axis=-1, keepdims=True) + 1e-06)
    return tensor * scale, scale


def strict_lower(rows, cols):
    return lax.broadcasted_iota(jnp.int32, (rows, cols), 0) > lax.broadcasted_iota(
        jnp.int32, (rows, cols), 1
    )


def tri_inverse(keys):
    heads, rows, size = keys.shape
    leaves = rows // LEAF
    leaf_keys = keys.reshape(heads, leaves, LEAF, size)
    gram = mm("hpid,hpjd->hpij", leaf_keys, leaf_keys)
    power = jnp.where(strict_lower(LEAF, LEAF), -2.0 * gram, 0.0)
    eye = jnp.eye(LEAF, dtype=jnp.float32)
    inverse = eye + power
    reach = 2
    while reach < LEAF:
        power = mm("hpij,hpjk->hpik", power, power)
        inverse = inverse + mm("hpij,hpjk->hpik", inverse, power)
        reach *= 2
    span = LEAF
    while span < rows:
        pairs = rows // (2 * span)
        blocks = inverse.reshape(heads, pairs, 2, span, span)
        upper_inv = blocks[:, :, 0]
        lower_inv = blocks[:, :, 1]
        halves = keys.reshape(heads, pairs, 2, span, size)
        link = 2.0 * mm("hpid,hpjd->hpij", halves[:, :, 1], halves[:, :, 0])
        corner = -mm("hpij,hpjk->hpik", lower_inv, mm("hpij,hpjk->hpik", link, upper_inv))
        top = jnp.concatenate([upper_inv, jnp.zeros_like(upper_inv)], axis=3)
        bottom = jnp.concatenate([corner, lower_inv], axis=3)
        inverse = jnp.concatenate([top, bottom], axis=2)
        span *= 2
    return inverse.reshape(heads, rows, rows)


def chain_seq(transition, offset, local_cot):
    count = lax.axis_size("seq")
    right = [(i, i + 1) for i in range(count - 1)]
    left = [(i + 1, i) for i in range(count - 1)]
    fwd_sum, bwd_sum = offset, local_cot
    for hop in range(count - 1):
        got_sum = lax.ppermute(fwd_sum, "seq", right)
        got_cot = lax.ppermute(bwd_sum, "seq", left)
        if hop == count - 2:
            return got_sum, got_cot
        fwd_sum = mm("hij,hjk->hik", transition, got_sum) + offset
        bwd_sum = mm("hji,hjk->hik", transition, got_cot) + local_cot
    zero = jnp.zeros_like(offset)
    return zero, zero


def scan_seq(transition, offset, local_cot):
    count = lax.axis_size("seq")
    if count <= 4:
        return chain_seq(transition, offset, local_cot)
    fwd_map, fwd_sum = transition, offset
    bwd_map, bwd_sum = transition, local_cot
    shift = 1
    while shift < count:
        right = [(i, i + shift) for i in range(count - shift)]
        left = [(i + shift, i) for i in range(count - shift)]
        last = 2 * shift >= count
        if last:
            got_sum = lax.ppermute(fwd_sum, "seq", right)
            got_cot = lax.ppermute(bwd_sum, "seq", left)
        else:
            got_map, got_sum = lax.ppermute((fwd_map, fwd_sum), "seq", right)
            got_bmap, got_cot = lax.ppermute((bwd_map, bwd_sum), "seq", left)
        fwd_sum = mm("hij,hjk->hik", fwd_map, got_sum) + fwd_sum
        bwd_sum = mm("hji,hjk->hik", bwd_map, got_cot) + bwd_sum
        if not last:
            fwd_map = mm("hij,hjk->hik", fwd_map, got_map)
            bwd_map = mm("hij,hjk->hik", got_bmap, bwd_map)
        shift *= 2
    state_in = lax.ppermute(fwd_sum, "seq", [(i, i + 1) for i in range(count - 1)])
    end_cot = lax.ppermute(bwd_sum, "seq", [(i + 1, i) for i in range(count - 1)])
    return state_in, end_cot


def local(queries, reflect_keys, write_values, out_cotangent):
    tok_count, heads_here, head_size = queries.shape
    rows = 2 * tok_count
    q_raw = queries.astype(jnp.float32).transpose(1, 0, 2)
    cot = out_cotangent.astype(jnp.float32).transpose(1, 0, 2)
    k_raw = reflect_keys.astype(jnp.float32).reshape(rows, heads_here, head_size).transpose(1, 0, 2)
    vals = write_values.astype(jnp.float32).reshape(rows, heads_here, head_size).transpose(1, 0, 2)
    qn, q_scale = unit_rows(q_raw)
    kn, k_scale = unit_rows(k_raw)

    inverse = tri_inverse(kn)
    proj = mh("hij,hjd->hid", inverse, kn)
    upd_v = mh("hij,hjd->hid", inverse, vals)
    tok_ids = lax.broadcasted_iota(jnp.int32, (tok_count, rows), 0)
    sub_ids = lax.broadcasted_iota(jnp.int32, (tok_count, rows), 1)
    visible = sub_ids <= 2 * tok_ids + 1
    scores = jnp.where(visible, 2.0 * mh("hid,hjd->hij", qn, kn), 0.0)
    read_map = qn - mh("hij,hjd->hid", scores, proj)
    own_out = mh("hij,hjd->hid", scores, upd_v)
    eye = jnp.eye(head_size, dtype=jnp.float32)
    transition = eye - 2.0 * mh("hjd,hjw->hdw", kn, proj)
    offset = 2.0 * mh("hjd,hjw->hdw", kn, upd_v)
    local_cot = mh("hld,hlw->hdw", read_map, cot)

    state_in, end_cot = scan_seq(transition, offset, local_cot)

    produced = mh("hld,hdw->lhw", read_map, state_in) + own_out.transpose(1, 0, 2)
    updates = upd_v - mh("hjd,hdw->hjw", proj, state_in)
    d_upd = mh("hij,hiw->hjw", scores, cot) + 2.0 * mh("hjd,hdw->hjw", kn, end_cot)
    d_w = mh("hij,hiw->jhw", inverse, d_upd)
    touch = jnp.where(visible, mh("hiw,hjw->hij", cot, updates), 0.0)
    d_qn = mh("hiw,hdw->ihd", cot, state_in) + 2.0 * mh("hij,hjd->ihd", touch, kn)
    gram_cot = jnp.where(strict_lower(rows, rows), -2.0 * mh("ihw,hjw->hij", d_w, updates), 0.0)
    d_kn = (
        2.0 * mh("hij,hid->jhd", touch, qn)
        + 2.0 * mh("hjw,hdw->jhd", updates, end_cot)
        - mh("jhw,hdw->jhd", d_w, state_in)
        + mh("hij,hjd->ihd", gram_cot, kn)
        + mh("hji,hjd->ihd", gram_cot, kn)
    )
    qn_t, q_scale_t = qn.transpose(1, 0, 2), q_scale.transpose(1, 0, 2)
    kn_t, k_scale_t = kn.transpose(1, 0, 2), k_scale.transpose(1, 0, 2)
    d_q = q_scale_t * (d_qn - jnp.sum(qn_t * d_qn, axis=-1, keepdims=True) * qn_t)
    d_k = k_scale_t * (d_kn - jnp.sum(kn_t * d_kn, axis=-1, keepdims=True) * kn_t)

    def pair_major(tensor):
        return tensor.reshape(tok_count, 2, heads_here, head_size).astype(jnp.bfloat16)

    return (
        produced.astype(jnp.bfloat16),
        d_q.astype(jnp.bfloat16),
        pair_major(d_k),
        pair_major(d_w),
    )


def solution(mesh):
    in_specs = (
        P(("groups", "seq"), "head", None),
        P(("groups", "seq"), None, "head", None),
        P(("groups", "seq"), None, "head", None),
        P(("groups", "seq"), "head", None),
    )
    out_specs = (
        P(("groups", "seq"), "head", None),
        P(("groups", "seq"), "head", None),
        P(("groups", "seq"), None, "head", None),
        P(("groups", "seq"), None, "head", None),
    )
    return jax.shard_map(local, mesh=mesh, in_specs=in_specs, out_specs=out_specs, check_vma=False)
```

```python
import jax
import jax.numpy as jnp
from jax import lax
from jax.sharding import PartitionSpec as P

highest = lax.Precision.HIGHEST
LEAF = 16


def mm(spec, *operands):
    return jnp.einsum(spec, *operands, precision=highest)


def mh(spec, *operands):
    return jnp.einsum(spec, *operands, precision=lax.Precision.HIGH)


def unit_rows(tensor):
    scale = lax.rsqrt(jnp.sum(tensor * tensor, axis=-1, keepdims=True) + 1e-06)
    return tensor * scale, scale


def strict_lower(rows, cols):
    return lax.broadcasted_iota(jnp.int32, (rows, cols), 0) > lax.broadcasted_iota(
        jnp.int32, (rows, cols), 1
    )


def tri_inverse(keys):
    heads, rows, size = keys.shape
    leaves = rows // LEAF
    leaf_keys = keys.reshape(heads, leaves, LEAF, size)
    gram = mm("hpid,hpjd->hpij", leaf_keys, leaf_keys)
    power = jnp.where(strict_lower(LEAF, LEAF), -2.0 * gram, 0.0)
    eye = jnp.eye(LEAF, dtype=jnp.float32)
    inverse = eye + power
    reach = 2
    while reach < LEAF:
        power = mm("hpij,hpjk->hpik", power, power)
        inverse = inverse + mm("hpij,hpjk->hpik", inverse, power)
        reach *= 2
    span = LEAF
    while span < rows:
        pairs = rows // (2 * span)
        blocks = inverse.reshape(heads, pairs, 2, span, span)
        upper_inv = blocks[:, :, 0]
        lower_inv = blocks[:, :, 1]
        halves = keys.reshape(heads, pairs, 2, span, size)
        link = 2.0 * mm("hpid,hpjd->hpij", halves[:, :, 1], halves[:, :, 0])
        corner = -mm("hpij,hpjk->hpik", lower_inv, mm("hpij,hpjk->hpik", link, upper_inv))
        top = jnp.concatenate([upper_inv, jnp.zeros_like(upper_inv)], axis=3)
        bottom = jnp.concatenate([corner, lower_inv], axis=3)
        inverse = jnp.concatenate([top, bottom], axis=2)
        span *= 2
    return inverse.reshape(heads, rows, rows)


def chain_seq(transition, offset, local_cot):
    count = lax.axis_size("seq")
    right = [(i, i + 1) for i in range(count - 1)]
    left = [(i + 1, i) for i in range(count - 1)]
    fwd_sum, bwd_sum = offset, local_cot
    for hop in range(count - 1):
        got_sum = lax.ppermute(fwd_sum, "seq", right)
        got_cot = lax.ppermute(bwd_sum, "seq", left)
        if hop == count - 2:
            return got_sum, got_cot
        fwd_sum = mh("hij,hjk->hik", transition, got_sum) + offset
        bwd_sum = mh("hji,hjk->hik", transition, got_cot) + local_cot
    zero = jnp.zeros_like(offset)
    return zero, zero


def scan_seq(transition, offset, local_cot):
    count = lax.axis_size("seq")
    if count <= 4:
        return chain_seq(transition, offset, local_cot)
    fwd_map, fwd_sum = transition, offset
    bwd_map, bwd_sum = transition, local_cot
    shift = 1
    while shift < count:
        right = [(i, i + shift) for i in range(count - shift)]
        left = [(i + shift, i) for i in range(count - shift)]
        last = 2 * shift >= count
        if last:
            got_sum = lax.ppermute(fwd_sum, "seq", right)
            got_cot = lax.ppermute(bwd_sum, "seq", left)
        else:
            got_map, got_sum = lax.ppermute((fwd_map, fwd_sum), "seq", right)
            got_bmap, got_cot = lax.ppermute((bwd_map, bwd_sum), "seq", left)
        fwd_sum = mm("hij,hjk->hik", fwd_map, got_sum) + fwd_sum
        bwd_sum = mm("hji,hjk->hik", bwd_map, got_cot) + bwd_sum
        if not last:
            fwd_map = mm("hij,hjk->hik", fwd_map, got_map)
            bwd_map = mm("hij,hjk->hik", got_bmap, bwd_map)
        shift *= 2
    state_in = lax.ppermute(fwd_sum, "seq", [(i, i + 1) for i in range(count - 1)])
    end_cot = lax.ppermute(bwd_sum, "seq", [(i + 1, i) for i in range(count - 1)])
    return state_in, end_cot


def local(queries, reflect_keys, write_values, out_cotangent):
    tok_count, heads_here, head_size = queries.shape
    rows = 2 * tok_count
    q_raw = queries.astype(jnp.float32).transpose(1, 0, 2)
    cot = out_cotangent.astype(jnp.float32).transpose(1, 0, 2)
    k_raw = reflect_keys.astype(jnp.float32).reshape(rows, heads_here, head_size).transpose(1, 0, 2)
    vals = write_values.astype(jnp.float32).reshape(rows, heads_here, head_size).transpose(1, 0, 2)
    qn, q_scale = unit_rows(q_raw)
    kn, k_scale = unit_rows(k_raw)

    inverse = tri_inverse(kn)
    proj = mh("hij,hjd->hid", inverse, kn)
    upd_v = mh("hij,hjd->hid", inverse, vals)
    tok_ids = lax.broadcasted_iota(jnp.int32, (tok_count, rows), 0)
    sub_ids = lax.broadcasted_iota(jnp.int32, (tok_count, rows), 1)
    visible = sub_ids <= 2 * tok_ids + 1
    scores = jnp.where(visible, 2.0 * mh("hid,hjd->hij", qn, kn), 0.0)
    read_map = qn - mh("hij,hjd->hid", scores, proj)
    own_out = mh("hij,hjd->hid", scores, upd_v)
    eye = jnp.eye(head_size, dtype=jnp.float32)
    transition = eye - 2.0 * mh("hjd,hjw->hdw", kn, proj)
    offset = 2.0 * mh("hjd,hjw->hdw", kn, upd_v)
    local_cot = mh("hld,hlw->hdw", read_map, cot)

    state_in, end_cot = scan_seq(transition, offset, local_cot)

    produced = mh("hld,hdw->hlw", read_map, state_in) + own_out
    updates = upd_v - mh("hjd,hdw->hjw", proj, state_in)
    d_upd = mh("hij,hiw->hjw", scores, cot) + 2.0 * mh("hjd,hdw->hjw", kn, end_cot)
    d_w = mh("hij,hiw->hjw", inverse, d_upd)
    touch = jnp.where(visible, mh("hiw,hjw->hij", cot, updates), 0.0)
    d_qn = mh("hiw,hdw->hid", cot, state_in) + 2.0 * mh("hij,hjd->hid", touch, kn)
    gram_cot = jnp.where(strict_lower(rows, rows), -2.0 * mh("hiw,hjw->hij", d_w, updates), 0.0)
    d_kn = (
        2.0 * mh("hij,hid->hjd", touch, qn)
        + 2.0 * mh("hjw,hdw->hjd", updates, end_cot)
        - mh("hjw,hdw->hjd", d_w, state_in)
        + mh("hij,hjd->hid", gram_cot, kn)
        + mh("hji,hjd->hid", gram_cot, kn)
    )
    d_q = q_scale * (d_qn - jnp.sum(qn * d_qn, axis=-1, keepdims=True) * qn)
    d_k = k_scale * (d_kn - jnp.sum(kn * d_kn, axis=-1, keepdims=True) * kn)

    def token_major(tensor):
        return tensor.transpose(1, 0, 2).astype(jnp.bfloat16)

    def pair_major(tensor):
        return (
            tensor.reshape(heads_here, tok_count, 2, head_size)
            .transpose(1, 2, 0, 3)
            .astype(jnp.bfloat16)
        )

    return (token_major(produced), token_major(d_q), pair_major(d_k), pair_major(d_w))


def solution(mesh):
    in_specs = (
        P(("groups", "seq"), "head", None),
        P(("groups", "seq"), None, "head", None),
        P(("groups", "seq"), None, "head", None),
        P(("groups", "seq"), "head", None),
    )
    out_specs = (
        P(("groups", "seq"), "head", None),
        P(("groups", "seq"), "head", None),
        P(("groups", "seq"), None, "head", None),
        P(("groups", "seq"), None, "head", None),
    )
    return jax.shard_map(local, mesh=mesh, in_specs=in_specs, out_specs=out_specs, check_vma=False)
```

```python
import jax
import jax.numpy as jnp
from jax import lax
from jax.sharding import PartitionSpec as P

highest = lax.Precision.HIGHEST
LEAF = 16


def mm(spec, *operands):
    return jnp.einsum(spec, *operands, precision=highest)


def mh(spec, *operands):
    return jnp.einsum(spec, *operands, precision=lax.Precision.HIGH)


def unit_rows(tensor):
    scale = lax.rsqrt(jnp.sum(tensor * tensor, axis=-1, keepdims=True) + 1e-06)
    return tensor * scale, scale


def strict_lower(rows, cols):
    return lax.broadcasted_iota(jnp.int32, (rows, cols), 0) > lax.broadcasted_iota(
        jnp.int32, (rows, cols), 1
    )


def tri_inverse(keys):
    heads, rows, size = keys.shape
    leaves = rows // LEAF
    leaf_keys = keys.reshape(heads, leaves, LEAF, size)
    gram = mm("hpid,hpjd->hpij", leaf_keys, leaf_keys)
    power = jnp.where(strict_lower(LEAF, LEAF), -2.0 * gram, 0.0)
    eye = jnp.eye(LEAF, dtype=jnp.float32)
    inverse = eye + power
    reach = 2
    while reach < LEAF:
        power = mm("hpij,hpjk->hpik", power, power)
        inverse = inverse + mm("hpij,hpjk->hpik", inverse, power)
        reach *= 2
    span = LEAF
    while span < rows:
        pairs = rows // (2 * span)
        blocks = inverse.reshape(heads, pairs, 2, span, span)
        upper_inv = blocks[:, :, 0]
        lower_inv = blocks[:, :, 1]
        halves = keys.reshape(heads, pairs, 2, span, size)
        link = 2.0 * mm("hpid,hpjd->hpij", halves[:, :, 1], halves[:, :, 0])
        corner = -mm("hpij,hpjk->hpik", lower_inv, mm("hpij,hpjk->hpik", link, upper_inv))
        top = jnp.concatenate([upper_inv, jnp.zeros_like(upper_inv)], axis=3)
        bottom = jnp.concatenate([corner, lower_inv], axis=3)
        inverse = jnp.concatenate([top, bottom], axis=2)
        span *= 2
    return inverse.reshape(heads, rows, rows)


def chain_seq(transition, offset, local_cot):
    count = lax.axis_size("seq")
    right = [(i, i + 1) for i in range(count - 1)]
    left = [(i + 1, i) for i in range(count - 1)]
    fwd_sum, bwd_sum = offset, local_cot
    for hop in range(count - 1):
        got_sum = lax.ppermute(fwd_sum, "seq", right)
        got_cot = lax.ppermute(bwd_sum, "seq", left)
        if hop == count - 2:
            return got_sum, got_cot
        fwd_sum = mh("hij,hjk->hik", transition, got_sum) + offset
        bwd_sum = mh("hji,hjk->hik", transition, got_cot) + local_cot
    zero = jnp.zeros_like(offset)
    return zero, zero


def scan_seq(transition, offset, local_cot):
    count = lax.axis_size("seq")
    if count <= 4:
        return chain_seq(transition, offset, local_cot)
    fwd_map, fwd_sum = transition, offset
    bwd_map, bwd_sum = transition, local_cot
    shift = 1
    while shift < count:
        right = [(i, i + shift) for i in range(count - shift)]
        left = [(i + shift, i) for i in range(count - shift)]
        last = 2 * shift >= count
        if last:
            got_sum = lax.ppermute(fwd_sum, "seq", right)
            got_cot = lax.ppermute(bwd_sum, "seq", left)
        else:
            got_map, got_sum = lax.ppermute((fwd_map, fwd_sum), "seq", right)
            got_bmap, got_cot = lax.ppermute((bwd_map, bwd_sum), "seq", left)
        fwd_sum = mm("hij,hjk->hik", fwd_map, got_sum) + fwd_sum
        bwd_sum = mm("hji,hjk->hik", bwd_map, got_cot) + bwd_sum
        if not last:
            fwd_map = mm("hij,hjk->hik", fwd_map, got_map)
            bwd_map = mm("hij,hjk->hik", got_bmap, bwd_map)
        shift *= 2
    state_in = lax.ppermute(fwd_sum, "seq", [(i, i + 1) for i in range(count - 1)])
    end_cot = lax.ppermute(bwd_sum, "seq", [(i + 1, i) for i in range(count - 1)])
    return state_in, end_cot


def local(queries, reflect_keys, write_values, out_cotangent):
    tok_count, heads_here, head_size = queries.shape
    rows = 2 * tok_count
    q_raw = queries.astype(jnp.float32).transpose(1, 0, 2)
    cot = out_cotangent.astype(jnp.float32).transpose(1, 0, 2)
    k_raw = reflect_keys.astype(jnp.float32).reshape(rows, heads_here, head_size).transpose(1, 0, 2)
    vals = write_values.astype(jnp.float32).reshape(rows, heads_here, head_size).transpose(1, 0, 2)
    qn, q_scale = unit_rows(q_raw)
    kn, k_scale = unit_rows(k_raw)

    inverse = tri_inverse(kn)
    proj = mh("hij,hjd->hid", inverse, kn)
    upd_v = mh("hij,hjd->hid", inverse, vals)
    tok_ids = lax.broadcasted_iota(jnp.int32, (tok_count, rows), 0)
    sub_ids = lax.broadcasted_iota(jnp.int32, (tok_count, rows), 1)
    visible = sub_ids <= 2 * tok_ids + 1
    scores = jnp.where(visible, 2.0 * mh("hid,hjd->hij", qn, kn), 0.0)
    read_map = qn - mh("hij,hjd->hid", scores, proj)
    own_out = mh("hij,hjd->hid", scores, upd_v)
    eye = jnp.eye(head_size, dtype=jnp.float32)
    transition = eye - 2.0 * mh("hjd,hjw->hdw", kn, proj)
    offset = 2.0 * mh("hjd,hjw->hdw", kn, upd_v)
    seen_cot = mh("hij,hiw->hjw", scores, cot)
    local_cot = mh("hld,hlw->hdw", qn, cot) - mh("hjd,hjw->hdw", proj, seen_cot)

    state_in, end_cot = scan_seq(transition, offset, local_cot)

    produced = mh("hld,hdw->hlw", read_map, state_in) + own_out
    updates = upd_v - mh("hjd,hdw->hjw", proj, state_in)
    d_upd = seen_cot + 2.0 * mh("hjd,hdw->hjw", kn, end_cot)
    d_w = mh("hij,hiw->hjw", inverse, d_upd)
    touch = jnp.where(visible, mh("hiw,hjw->hij", cot, updates), 0.0)
    d_qn = mh("hiw,hdw->hid", cot, state_in) + 2.0 * mh("hij,hjd->hid", touch, kn)
    gram_cot = jnp.where(strict_lower(rows, rows), -2.0 * mh("hiw,hjw->hij", d_w, updates), 0.0)
    d_kn = (
        2.0 * mh("hij,hid->hjd", touch, qn)
        + 2.0 * mh("hjw,hdw->hjd", updates, end_cot)
        - mh("hjw,hdw->hjd", d_w, state_in)
        + mh("hij,hjd->hid", gram_cot, kn)
        + mh("hji,hjd->hid", gram_cot, kn)
    )
    d_q = q_scale * (d_qn - jnp.sum(qn * d_qn, axis=-1, keepdims=True) * qn)
    d_k = k_scale * (d_kn - jnp.sum(kn * d_kn, axis=-1, keepdims=True) * kn)

    def token_major(tensor):
        return tensor.transpose(1, 0, 2).astype(jnp.bfloat16)

    def pair_major(tensor):
        return (
            tensor.reshape(heads_here, tok_count, 2, head_size)
            .transpose(1, 2, 0, 3)
            .astype(jnp.bfloat16)
        )

    return (token_major(produced), token_major(d_q), pair_major(d_k), pair_major(d_w))


def solution(mesh):
    in_specs = (
        P(("groups", "seq"), "head", None),
        P(("groups", "seq"), None, "head", None),
        P(("groups", "seq"), None, "head", None),
        P(("groups", "seq"), "head", None),
    )
    out_specs = (
        P(("groups", "seq"), "head", None),
        P(("groups", "seq"), "head", None),
        P(("groups", "seq"), None, "head", None),
        P(("groups", "seq"), None, "head", None),
    )
    return jax.shard_map(local, mesh=mesh, in_specs=in_specs, out_specs=out_specs, check_vma=False)
```

```python
import jax
import jax.numpy as jnp
from jax import lax
from jax.sharding import PartitionSpec as P

highest = lax.Precision.HIGHEST
LEAF = 8


def mm(spec, *operands):
    return jnp.einsum(spec, *operands, precision=highest)


def mh(spec, *operands):
    return jnp.einsum(spec, *operands, precision=lax.Precision.HIGH)


def unit_rows(tensor):
    scale = lax.rsqrt(jnp.sum(tensor * tensor, axis=-1, keepdims=True) + 1e-06)
    return tensor * scale, scale


def strict_lower(rows, cols):
    return lax.broadcasted_iota(jnp.int32, (rows, cols), 0) > lax.broadcasted_iota(
        jnp.int32, (rows, cols), 1
    )


def tri_inverse(keys):
    heads, rows, size = keys.shape
    leaves = rows // LEAF
    leaf_keys = keys.reshape(heads, leaves, LEAF, size)
    gram = mm("hpid,hpjd->hpij", leaf_keys, leaf_keys)
    power = jnp.where(strict_lower(LEAF, LEAF), -2.0 * gram, 0.0)
    eye = jnp.eye(LEAF, dtype=jnp.float32)
    inverse = eye + power
    reach = 2
    while reach < LEAF:
        power = mm("hpij,hpjk->hpik", power, power)
        inverse = inverse + mm("hpij,hpjk->hpik", inverse, power)
        reach *= 2
    span = LEAF
    while span < rows:
        pairs = rows // (2 * span)
        blocks = inverse.reshape(heads, pairs, 2, span, span)
        upper_inv = blocks[:, :, 0]
        lower_inv = blocks[:, :, 1]
        halves = keys.reshape(heads, pairs, 2, span, size)
        link = 2.0 * mm("hpid,hpjd->hpij", halves[:, :, 1], halves[:, :, 0])
        corner = -mm("hpij,hpjk->hpik", lower_inv, mm("hpij,hpjk->hpik", link, upper_inv))
        top = jnp.concatenate([upper_inv, jnp.zeros_like(upper_inv)], axis=3)
        bottom = jnp.concatenate([corner, lower_inv], axis=3)
        inverse = jnp.concatenate([top, bottom], axis=2)
        span *= 2
    return inverse.reshape(heads, rows, rows)


def chain_seq(transition, offset, local_cot):
    count = lax.axis_size("seq")
    right = [(i, i + 1) for i in range(count - 1)]
    left = [(i + 1, i) for i in range(count - 1)]
    fwd_sum, bwd_sum = offset, local_cot
    for hop in range(count - 1):
        got_sum = lax.ppermute(fwd_sum, "seq", right)
        got_cot = lax.ppermute(bwd_sum, "seq", left)
        if hop == count - 2:
            return got_sum, got_cot
        fwd_sum = mh("hij,hjk->hik", transition, got_sum) + offset
        bwd_sum = mh("hji,hjk->hik", transition, got_cot) + local_cot
    zero = jnp.zeros_like(offset)
    return zero, zero


def scan_seq(transition, offset, local_cot):
    count = lax.axis_size("seq")
    if count <= 4:
        return chain_seq(transition, offset, local_cot)
    fwd_map, fwd_sum = transition, offset
    bwd_map, bwd_sum = transition, local_cot
    shift = 1
    while shift < count:
        right = [(i, i + shift) for i in range(count - shift)]
        left = [(i + shift, i) for i in range(count - shift)]
        last = 2 * shift >= count
        if last:
            got_sum = lax.ppermute(fwd_sum, "seq", right)
            got_cot = lax.ppermute(bwd_sum, "seq", left)
        else:
            got_map, got_sum = lax.ppermute((fwd_map, fwd_sum), "seq", right)
            got_bmap, got_cot = lax.ppermute((bwd_map, bwd_sum), "seq", left)
        fwd_sum = mm("hij,hjk->hik", fwd_map, got_sum) + fwd_sum
        bwd_sum = mm("hji,hjk->hik", bwd_map, got_cot) + bwd_sum
        if not last:
            fwd_map = mm("hij,hjk->hik", fwd_map, got_map)
            bwd_map = mm("hij,hjk->hik", got_bmap, bwd_map)
        shift *= 2
    state_in = lax.ppermute(fwd_sum, "seq", [(i, i + 1) for i in range(count - 1)])
    end_cot = lax.ppermute(bwd_sum, "seq", [(i + 1, i) for i in range(count - 1)])
    return state_in, end_cot


def local(queries, reflect_keys, write_values, out_cotangent):
    tok_count, heads_here, head_size = queries.shape
    rows = 2 * tok_count
    q_raw = queries.astype(jnp.float32).transpose(1, 0, 2)
    cot = out_cotangent.astype(jnp.float32).transpose(1, 0, 2)
    k_raw = reflect_keys.astype(jnp.float32).reshape(rows, heads_here, head_size).transpose(1, 0, 2)
    vals = write_values.astype(jnp.float32).reshape(rows, heads_here, head_size).transpose(1, 0, 2)
    qn, q_scale = unit_rows(q_raw)
    kn, k_scale = unit_rows(k_raw)

    inverse = tri_inverse(kn)
    proj = mh("hij,hjd->hid", inverse, kn)
    upd_v = mh("hij,hjd->hid", inverse, vals)
    tok_ids = lax.broadcasted_iota(jnp.int32, (tok_count, rows), 0)
    sub_ids = lax.broadcasted_iota(jnp.int32, (tok_count, rows), 1)
    visible = sub_ids <= 2 * tok_ids + 1
    scores = jnp.where(visible, 2.0 * mh("hid,hjd->hij", qn, kn), 0.0)
    read_map = qn - mh("hij,hjd->hid", scores, proj)
    own_out = mh("hij,hjd->hid", scores, upd_v)
    eye = jnp.eye(head_size, dtype=jnp.float32)
    transition = eye - 2.0 * mh("hjd,hjw->hdw", kn, proj)
    offset = 2.0 * mh("hjd,hjw->hdw", kn, upd_v)
    local_cot = mh("hld,hlw->hdw", read_map, cot)

    state_in, end_cot = scan_seq(transition, offset, local_cot)

    produced = mh("hld,hdw->hlw", read_map, state_in) + own_out
    updates = upd_v - mh("hjd,hdw->hjw", proj, state_in)
    d_upd = mh("hij,hiw->hjw", scores, cot) + 2.0 * mh("hjd,hdw->hjw", kn, end_cot)
    d_w = mh("hij,hiw->hjw", inverse, d_upd)
    touch = jnp.where(visible, mh("hiw,hjw->hij", cot, updates), 0.0)
    d_qn = mh("hiw,hdw->hid", cot, state_in) + 2.0 * mh("hij,hjd->hid", touch, kn)
    gram_cot = jnp.where(strict_lower(rows, rows), -2.0 * mh("hiw,hjw->hij", d_w, updates), 0.0)
    d_kn = (
        2.0 * mh("hij,hid->hjd", touch, qn)
        + 2.0 * mh("hjw,hdw->hjd", updates, end_cot)
        - mh("hjw,hdw->hjd", d_w, state_in)
        + mh("hij,hjd->hid", gram_cot, kn)
        + mh("hji,hjd->hid", gram_cot, kn)
    )
    d_q = q_scale * (d_qn - jnp.sum(qn * d_qn, axis=-1, keepdims=True) * qn)
    d_k = k_scale * (d_kn - jnp.sum(kn * d_kn, axis=-1, keepdims=True) * kn)

    def token_major(tensor):
        return tensor.transpose(1, 0, 2).astype(jnp.bfloat16)

    def pair_major(tensor):
        return (
            tensor.reshape(heads_here, tok_count, 2, head_size)
            .transpose(1, 2, 0, 3)
            .astype(jnp.bfloat16)
        )

    return (token_major(produced), token_major(d_q), pair_major(d_k), pair_major(d_w))


def solution(mesh):
    in_specs = (
        P(("groups", "seq"), "head", None),
        P(("groups", "seq"), None, "head", None),
        P(("groups", "seq"), None, "head", None),
        P(("groups", "seq"), "head", None),
    )
    out_specs = (
        P(("groups", "seq"), "head", None),
        P(("groups", "seq"), "head", None),
        P(("groups", "seq"), None, "head", None),
        P(("groups", "seq"), None, "head", None),
    )
    return jax.shard_map(local, mesh=mesh, in_specs=in_specs, out_specs=out_specs, check_vma=False)
```

```python
import jax
import jax.numpy as jnp
from jax import lax
from jax.sharding import PartitionSpec as P

highest = lax.Precision.HIGHEST
LEAF = 16


def mm(spec, *operands):
    return jnp.einsum(spec, *operands, precision=highest)


def mh(spec, *operands):
    return jnp.einsum(spec, *operands, precision=lax.Precision.HIGH)


def unit_rows(tensor):
    scale = lax.rsqrt(jnp.sum(tensor * tensor, axis=-1, keepdims=True) + 1e-06)
    return tensor * scale, scale


def strict_lower(rows, cols):
    return lax.broadcasted_iota(jnp.int32, (rows, cols), 0) > lax.broadcasted_iota(
        jnp.int32, (rows, cols), 1
    )


def tri_inverse(keys):
    heads, rows, size = keys.shape
    leaves = rows // LEAF
    leaf_keys = keys.reshape(heads, leaves, LEAF, size)
    gram = mm("hpid,hpjd->hpij", leaf_keys, leaf_keys)
    power = jnp.where(strict_lower(LEAF, LEAF), -2.0 * gram, 0.0)
    eye = jnp.eye(LEAF, dtype=jnp.float32)
    inverse = eye + power
    reach = 2
    while reach < LEAF:
        power = mh("hpij,hpjk->hpik", power, power)
        inverse = inverse + mh("hpij,hpjk->hpik", inverse, power)
        reach *= 2
    span = LEAF
    while span < rows:
        pairs = rows // (2 * span)
        blocks = inverse.reshape(heads, pairs, 2, span, span)
        upper_inv = blocks[:, :, 0]
        lower_inv = blocks[:, :, 1]
        halves = keys.reshape(heads, pairs, 2, span, size)
        link = 2.0 * mm("hpid,hpjd->hpij", halves[:, :, 1], halves[:, :, 0])
        corner = -mm("hpij,hpjk->hpik", lower_inv, mm("hpij,hpjk->hpik", link, upper_inv))
        top = jnp.concatenate([upper_inv, jnp.zeros_like(upper_inv)], axis=3)
        bottom = jnp.concatenate([corner, lower_inv], axis=3)
        inverse = jnp.concatenate([top, bottom], axis=2)
        span *= 2
    return inverse.reshape(heads, rows, rows)


def chain_seq(transition, offset, local_cot):
    count = lax.axis_size("seq")
    right = [(i, i + 1) for i in range(count - 1)]
    left = [(i + 1, i) for i in range(count - 1)]
    fwd_sum, bwd_sum = offset, local_cot
    for hop in range(count - 1):
        got_sum = lax.ppermute(fwd_sum, "seq", right)
        got_cot = lax.ppermute(bwd_sum, "seq", left)
        if hop == count - 2:
            return got_sum, got_cot
        fwd_sum = mh("hij,hjk->hik", transition, got_sum) + offset
        bwd_sum = mh("hji,hjk->hik", transition, got_cot) + local_cot
    zero = jnp.zeros_like(offset)
    return zero, zero


def scan_seq(transition, offset, local_cot):
    count = lax.axis_size("seq")
    if count <= 4:
        return chain_seq(transition, offset, local_cot)
    fwd_map, fwd_sum = transition, offset
    bwd_map, bwd_sum = transition, local_cot
    shift = 1
    while shift < count:
        right = [(i, i + shift) for i in range(count - shift)]
        left = [(i + shift, i) for i in range(count - shift)]
        last = 2 * shift >= count
        if last:
            got_sum = lax.ppermute(fwd_sum, "seq", right)
            got_cot = lax.ppermute(bwd_sum, "seq", left)
        else:
            got_map, got_sum = lax.ppermute((fwd_map, fwd_sum), "seq", right)
            got_bmap, got_cot = lax.ppermute((bwd_map, bwd_sum), "seq", left)
        fwd_sum = mm("hij,hjk->hik", fwd_map, got_sum) + fwd_sum
        bwd_sum = mm("hji,hjk->hik", bwd_map, got_cot) + bwd_sum
        if not last:
            fwd_map = mm("hij,hjk->hik", fwd_map, got_map)
            bwd_map = mm("hij,hjk->hik", got_bmap, bwd_map)
        shift *= 2
    state_in = lax.ppermute(fwd_sum, "seq", [(i, i + 1) for i in range(count - 1)])
    end_cot = lax.ppermute(bwd_sum, "seq", [(i + 1, i) for i in range(count - 1)])
    return state_in, end_cot


def local(queries, reflect_keys, write_values, out_cotangent):
    tok_count, heads_here, head_size = queries.shape
    rows = 2 * tok_count
    q_raw = queries.astype(jnp.float32).transpose(1, 0, 2)
    cot = out_cotangent.astype(jnp.float32).transpose(1, 0, 2)
    k_raw = reflect_keys.astype(jnp.float32).reshape(rows, heads_here, head_size).transpose(1, 0, 2)
    vals = write_values.astype(jnp.float32).reshape(rows, heads_here, head_size).transpose(1, 0, 2)
    qn, q_scale = unit_rows(q_raw)
    kn, k_scale = unit_rows(k_raw)

    inverse = tri_inverse(kn)
    proj = mh("hij,hjd->hid", inverse, kn)
    upd_v = mh("hij,hjd->hid", inverse, vals)
    tok_ids = lax.broadcasted_iota(jnp.int32, (tok_count, rows), 0)
    sub_ids = lax.broadcasted_iota(jnp.int32, (tok_count, rows), 1)
    visible = sub_ids <= 2 * tok_ids + 1
    scores = jnp.where(visible, 2.0 * mh("hid,hjd->hij", qn, kn), 0.0)
    read_map = qn - mh("hij,hjd->hid", scores, proj)
    own_out = mh("hij,hjd->hid", scores, upd_v)
    eye = jnp.eye(head_size, dtype=jnp.float32)
    transition = eye - 2.0 * mh("hjd,hjw->hdw", kn, proj)
    offset = 2.0 * mh("hjd,hjw->hdw", kn, upd_v)
    local_cot = mh("hld,hlw->hdw", read_map, cot)

    state_in, end_cot = scan_seq(transition, offset, local_cot)

    produced = mh("hld,hdw->hlw", read_map, state_in) + own_out
    updates = upd_v - mh("hjd,hdw->hjw", proj, state_in)
    d_upd = mh("hij,hiw->hjw", scores, cot) + 2.0 * mh("hjd,hdw->hjw", kn, end_cot)
    d_w = mh("hij,hiw->hjw", inverse, d_upd)
    touch = jnp.where(visible, mh("hiw,hjw->hij", cot, updates), 0.0)
    d_qn = mh("hiw,hdw->hid", cot, state_in) + 2.0 * mh("hij,hjd->hid", touch, kn)
    gram_cot = jnp.where(strict_lower(rows, rows), -2.0 * mh("hiw,hjw->hij", d_w, updates), 0.0)
    d_kn = (
        2.0 * mh("hij,hid->hjd", touch, qn)
        + 2.0 * mh("hjw,hdw->hjd", updates, end_cot)
        - mh("hjw,hdw->hjd", d_w, state_in)
        + mh("hij,hjd->hid", gram_cot, kn)
        + mh("hji,hjd->hid", gram_cot, kn)
    )
    d_q = q_scale * (d_qn - jnp.sum(qn * d_qn, axis=-1, keepdims=True) * qn)
    d_k = k_scale * (d_kn - jnp.sum(kn * d_kn, axis=-1, keepdims=True) * kn)

    def token_major(tensor):
        return tensor.transpose(1, 0, 2).astype(jnp.bfloat16)

    def pair_major(tensor):
        return (
            tensor.reshape(heads_here, tok_count, 2, head_size)
            .transpose(1, 2, 0, 3)
            .astype(jnp.bfloat16)
        )

    return (token_major(produced), token_major(d_q), pair_major(d_k), pair_major(d_w))


def solution(mesh):
    in_specs = (
        P(("groups", "seq"), "head", None),
        P(("groups", "seq"), None, "head", None),
        P(("groups", "seq"), None, "head", None),
        P(("groups", "seq"), "head", None),
    )
    out_specs = (
        P(("groups", "seq"), "head", None),
        P(("groups", "seq"), "head", None),
        P(("groups", "seq"), None, "head", None),
        P(("groups", "seq"), None, "head", None),
    )
    return jax.shard_map(local, mesh=mesh, in_specs=in_specs, out_specs=out_specs, check_vma=False)
```

```python
import jax
import jax.numpy as jnp
from jax import lax
from jax.sharding import PartitionSpec as P

highest = lax.Precision.HIGHEST
LEAF = 16


def mm(spec, *operands):
    return jnp.einsum(spec, *operands, precision=highest)


def mh(spec, *operands):
    return jnp.einsum(spec, *operands, precision=lax.Precision.HIGH)


def unit_rows(tensor):
    scale = lax.rsqrt(jnp.sum(tensor * tensor, axis=-1, keepdims=True) + 1e-06)
    return tensor * scale, scale


def strict_lower(rows, cols):
    return lax.broadcasted_iota(jnp.int32, (rows, cols), 0) > lax.broadcasted_iota(
        jnp.int32, (rows, cols), 1
    )


def tri_inverse(keys):
    heads, rows, size = keys.shape
    leaves = rows // LEAF
    leaf_keys = keys.reshape(heads, leaves, LEAF, size)
    gram = mh("hpid,hpjd->hpij", leaf_keys, leaf_keys)
    power = jnp.where(strict_lower(LEAF, LEAF), -2.0 * gram, 0.0)
    eye = jnp.eye(LEAF, dtype=jnp.float32)
    inverse = eye + power
    reach = 2
    while reach < LEAF:
        power = mh("hpij,hpjk->hpik", power, power)
        inverse = inverse + mh("hpij,hpjk->hpik", inverse, power)
        reach *= 2
    span = LEAF
    while span < rows:
        pairs = rows // (2 * span)
        blocks = inverse.reshape(heads, pairs, 2, span, span)
        upper_inv = blocks[:, :, 0]
        lower_inv = blocks[:, :, 1]
        halves = keys.reshape(heads, pairs, 2, span, size)
        link = 2.0 * mm("hpid,hpjd->hpij", halves[:, :, 1], halves[:, :, 0])
        corner = -mm("hpij,hpjk->hpik", lower_inv, mm("hpij,hpjk->hpik", link, upper_inv))
        top = jnp.concatenate([upper_inv, jnp.zeros_like(upper_inv)], axis=3)
        bottom = jnp.concatenate([corner, lower_inv], axis=3)
        inverse = jnp.concatenate([top, bottom], axis=2)
        span *= 2
    return inverse.reshape(heads, rows, rows)


def chain_seq(transition, offset, local_cot):
    count = lax.axis_size("seq")
    right = [(i, i + 1) for i in range(count - 1)]
    left = [(i + 1, i) for i in range(count - 1)]
    fwd_sum, bwd_sum = offset, local_cot
    for hop in range(count - 1):
        got_sum = lax.ppermute(fwd_sum, "seq", right)
        got_cot = lax.ppermute(bwd_sum, "seq", left)
        if hop == count - 2:
            return got_sum, got_cot
        fwd_sum = mh("hij,hjk->hik", transition, got_sum) + offset
        bwd_sum = mh("hji,hjk->hik", transition, got_cot) + local_cot
    zero = jnp.zeros_like(offset)
    return zero, zero


def scan_seq(transition, offset, local_cot):
    count = lax.axis_size("seq")
    if count <= 4:
        return chain_seq(transition, offset, local_cot)
    fwd_map, fwd_sum = transition, offset
    bwd_map, bwd_sum = transition, local_cot
    shift = 1
    while shift < count:
        right = [(i, i + shift) for i in range(count - shift)]
        left = [(i + shift, i) for i in range(count - shift)]
        last = 2 * shift >= count
        if last:
            got_sum = lax.ppermute(fwd_sum, "seq", right)
            got_cot = lax.ppermute(bwd_sum, "seq", left)
        else:
            got_map, got_sum = lax.ppermute((fwd_map, fwd_sum), "seq", right)
            got_bmap, got_cot = lax.ppermute((bwd_map, bwd_sum), "seq", left)
        fwd_sum = mm("hij,hjk->hik", fwd_map, got_sum) + fwd_sum
        bwd_sum = mm("hji,hjk->hik", bwd_map, got_cot) + bwd_sum
        if not last:
            fwd_map = mm("hij,hjk->hik", fwd_map, got_map)
            bwd_map = mm("hij,hjk->hik", got_bmap, bwd_map)
        shift *= 2
    state_in = lax.ppermute(fwd_sum, "seq", [(i, i + 1) for i in range(count - 1)])
    end_cot = lax.ppermute(bwd_sum, "seq", [(i + 1, i) for i in range(count - 1)])
    return state_in, end_cot


def local(queries, reflect_keys, write_values, out_cotangent):
    tok_count, heads_here, head_size = queries.shape
    rows = 2 * tok_count
    q_raw = queries.astype(jnp.float32).transpose(1, 0, 2)
    cot = out_cotangent.astype(jnp.float32).transpose(1, 0, 2)
    k_raw = reflect_keys.astype(jnp.float32).reshape(rows, heads_here, head_size).transpose(1, 0, 2)
    vals = write_values.astype(jnp.float32).reshape(rows, heads_here, head_size).transpose(1, 0, 2)
    qn, q_scale = unit_rows(q_raw)
    kn, k_scale = unit_rows(k_raw)

    inverse = tri_inverse(kn)
    proj = mh("hij,hjd->hid", inverse, kn)
    upd_v = mh("hij,hjd->hid", inverse, vals)
    tok_ids = lax.broadcasted_iota(jnp.int32, (tok_count, rows), 0)
    sub_ids = lax.broadcasted_iota(jnp.int32, (tok_count, rows), 1)
    visible = sub_ids <= 2 * tok_ids + 1
    scores = jnp.where(visible, 2.0 * mh("hid,hjd->hij", qn, kn), 0.0)
    read_map = qn - mh("hij,hjd->hid", scores, proj)
    own_out = mh("hij,hjd->hid", scores, upd_v)
    eye = jnp.eye(head_size, dtype=jnp.float32)
    transition = eye - 2.0 * mh("hjd,hjw->hdw", kn, proj)
    offset = 2.0 * mh("hjd,hjw->hdw", kn, upd_v)
    local_cot = mh("hld,hlw->hdw", read_map, cot)

    state_in, end_cot = scan_seq(transition, offset, local_cot)

    produced = mh("hld,hdw->hlw", read_map, state_in) + own_out
    updates = upd_v - mh("hjd,hdw->hjw", proj, state_in)
    d_upd = mh("hij,hiw->hjw", scores, cot) + 2.0 * mh("hjd,hdw->hjw", kn, end_cot)
    d_w = mh("hij,hiw->hjw", inverse, d_upd)
    touch = jnp.where(visible, mh("hiw,hjw->hij", cot, updates), 0.0)
    d_qn = mh("hiw,hdw->hid", cot, state_in) + 2.0 * mh("hij,hjd->hid", touch, kn)
    gram_cot = jnp.where(strict_lower(rows, rows), -2.0 * mh("hiw,hjw->hij", d_w, updates), 0.0)
    d_kn = (
        2.0 * mh("hij,hid->hjd", touch, qn)
        + 2.0 * mh("hjw,hdw->hjd", updates, end_cot)
        - mh("hjw,hdw->hjd", d_w, state_in)
        + mh("hij,hjd->hid", gram_cot, kn)
        + mh("hji,hjd->hid", gram_cot, kn)
    )
    d_q = q_scale * (d_qn - jnp.sum(qn * d_qn, axis=-1, keepdims=True) * qn)
    d_k = k_scale * (d_kn - jnp.sum(kn * d_kn, axis=-1, keepdims=True) * kn)

    def token_major(tensor):
        return tensor.transpose(1, 0, 2).astype(jnp.bfloat16)

    def pair_major(tensor):
        return (
            tensor.reshape(heads_here, tok_count, 2, head_size)
            .transpose(1, 2, 0, 3)
            .astype(jnp.bfloat16)
        )

    return (token_major(produced), token_major(d_q), pair_major(d_k), pair_major(d_w))


def solution(mesh):
    in_specs = (
        P(("groups", "seq"), "head", None),
        P(("groups", "seq"), None, "head", None),
        P(("groups", "seq"), None, "head", None),
        P(("groups", "seq"), "head", None),
    )
    out_specs = (
        P(("groups", "seq"), "head", None),
        P(("groups", "seq"), "head", None),
        P(("groups", "seq"), None, "head", None),
        P(("groups", "seq"), None, "head", None),
    )
    return jax.shard_map(local, mesh=mesh, in_specs=in_specs, out_specs=out_specs, check_vma=False)
```
